32 devices in a mesh: grp: 2 (over y), chan: 4 (over z), tile: 2 (over x), sub: 2 (over core).
Axes of the slice: x: 2, y: 2, z: 4, core: 2. Of those that a mesh axis runs over, the one named last changes fastest.
Arguments:
- dirty: bfloat16 [128, 32, 8, 128], P(('grp', 'chan'), None, ('tile', 'sub')), parts along dimension 0, may hold values from -6 to 6
- cotangent: bfloat16 [128, 32, 8, 128], P(('grp', 'chan'), None, ('tile', 'sub')), parts along dimension 0, may hold values from -6 to 6
- spatial_kernel: float32 [32, 25], replicated, may hold values from -1.25 to 1.25
- feature_mix: bfloat16 [32, 32], replicated, may hold values from -1 to 1
- spectral_kernel: bfloat16 [7, 32, 32], replicated, may hold values from -0.375 to 0.375
- freq_table: int32 [64], replicated, may hold values from 0 to 63, as said below
Outputs:
- restored: bfloat16 [128, 32, 8, 128], P(('grp', 'chan'), None, ('tile', 'sub')), parts along dimension 0
- dirty_grad: bfloat16 [128, 32, 8, 128], P(('grp', 'chan'), None, ('tile', 'sub')), parts along dimension 0
- spatial_grad: float32 [64, 25], P('grp'), parts along dimension 0
- mix_grad: float32 [64, 32], P('grp'), parts along dimension 0
- spectral_grad: float32 [14, 32, 32], P('grp'), parts along dimension 0
The draws below stay inside these ranges and needn't reach their ends.
There are 2 independent parts, one for each index of `grp`. The reference program is written for one: setup_inputs(seed, part) draws one part's arguments, and reference() takes and returns one part's arrays. A program takes and returns all parts, laid end to end along the dimension named above; an argument that names none is the same for every part. Nothing has to cross between parts.
Inputs may be any that keep to these rules, and one draw needn't show every extreme that they name: freq_table is a permutation of 0..63; the stored channels d * 16 to (d+1) * 16 - 1 hold exactly the frequencies m * 4 + d for m in 0..15, in any order.
All inputs are finite; a program needn't handle non-finite values.
Results may differ from the reference program's by a relative error of at most 0.0062.
Values may be sent and summed in bfloat16 or wider, within the bound.
No kernel may reach another device: no remote copies, remote signals or barrier semaphores. Data moves between devices by JAX's collectives and lax.ppermute only.
A program may use at most 64 MiB of HBM per device.

```python
import math
import jax
import jax.numpy as jnp
from jax import lax

F = 32
CH_DEV = 16
TAPS = 7
W = 128
C = 64
H = 8


def draw_freq_table(key, part):
    blocks = C // CH_DEV
    keys = jax.random.split(jax.random.fold_in(key, 17), blocks)
    perms = jax.vmap(lambda k: jax.random.permutation(k, CH_DEV))(keys)
    base = jnp.arange(blocks, dtype=jnp.int32)[:, None]
    return (perms.astype(jnp.int32) * blocks + base).reshape(C).astype(jnp.int32)


def block_scale(own_key, extent, cuts, least, top_value):
    factor_of = 1.0
    for dim, parts in cuts:
        heights = jax.random.uniform(jax.random.fold_in(jax.random.fold_in(own_key, 6), dim), (parts,), jnp.float32, least / len(cuts), top_value / len(cuts))
        factor_of = factor_of * jnp.repeat(jnp.exp(heights), extent[dim] // parts).reshape((-1,) + (1,) * (len(extent) - 1 - dim))
    return factor_of


def centred(key, extent, width, most, pieces=(), held_as=jnp.bfloat16):
    level = block_scale(key, extent, pieces, -0.22, 0.18) if pieces else 1.0
    drawn = jax.random.normal(key, extent, jnp.float32) * width * level
    return jnp.minimum(jnp.maximum(drawn, -most), most).astype(held_as)


def setup_inputs(seed: int = 0, part: int = 0) -> dict:
    streams_of = jax.random.split(jax.random.key(seed), 7)
    part_keys = jax.random.split(jax.random.fold_in(streams_of[6], part), 7)
    return {
        "dirty": centred(part_keys[0], (C, F, H, W), 1.0, 6.0, ((0, 4), (2, 4))),
        "cotangent": centred(part_keys[1], (C, F, H, W), 1.0, 6.0, ((0, 4), (2, 4))),
        "spatial_kernel": centred(streams_of[2], (F, 25), 25 ** -0.5, 1.25, (), jnp.float32),
        "feature_mix": centred(streams_of[3], (F, F), F ** -0.5, 1.0),
        "spectral_kernel": centred(streams_of[4], (TAPS, F, F), (TAPS * F) ** -0.5, 0.375),
        "freq_table": draw_freq_table(jax.random.fold_in(streams_of[6], 71), part),
    }


def spatial_forward(block, kernel):
    rows = block.shape[2]
    cols = block.shape[3]
    padded = jnp.pad(block.astype(jnp.float32), ((0, 0), (0, 0), (2, 2), (2, 2)))
    total = jnp.zeros(block.shape, jnp.float32)
    for i in range(5):
        for j in range(5):
            total = total + kernel[:, i * 5 + j][None, :, None, None] * padded[:, :, i:i + rows, j:j + cols]
    return total

def spectral_mix(hpad, gpad, kernel):
    taps = kernel.shape[0]
    reach = taps - 1
    count = hpad.shape[0] - reach
    hstack = jnp.stack([hpad[k:k + count] for k in range(taps)], 1).astype(jnp.float32)
    gstack = jnp.stack([gpad[reach - k:reach - k + count] for k in range(taps)], 1).astype(jnp.float32)
    kern = kernel.astype(jnp.float32)
    forward = jnp.einsum('kgf,qkfp->qgp', kern, hstack).astype(jnp.bfloat16)
    backward = jnp.einsum('kgf,qkgp->qfp', kern, gstack).astype(jnp.bfloat16)
    half = reach // 2
    center = gpad[half:half + count].astype(jnp.float32)
    grad = jnp.einsum('qgp,qkfp->kgf', center, hstack)
    return (forward, backward, grad)

def silu_slope(value):
    sig = jax.nn.sigmoid(value)
    return sig * (1.0 + value * (1.0 - sig))

def reference(dirty, cotangent, spatial_kernel, feature_mix, spectral_kernel, freq_table):
    blocks = C // CH_DEV
    mix32 = feature_mix.astype(jnp.float32)
    dirty_b = dirty.reshape(blocks, CH_DEV, F, H, W)
    cot_b = cotangent.reshape(blocks, CH_DEV, F, H, W)

    def forward_block(block):
        smooth = spatial_forward(block, spatial_kernel).astype(jnp.bfloat16)
        mixed = jnp.einsum('gf,cfhw->cghw', mix32, smooth.astype(jnp.float32))
        return (smooth, jax.nn.silu(mixed).astype(jnp.bfloat16))
    smooth_b, hidden_b = lax.map(forward_block, dirty_b)
    hidden = hidden_b.reshape(C, F, H, W)
    order = jnp.zeros((C,), jnp.int32).at[freq_table].set(jnp.arange(C, dtype=jnp.int32))
    half = (TAPS - 1) // 2

    def row_step(acc, pair):
        hrow, grow = pair
        hpad = jnp.pad(hrow[order], ((half, half), (0, 0), (0, 0)))
        gpad = jnp.pad(grow[order], ((half, half), (0, 0), (0, 0)))
        forward, backward, grad = spectral_mix(hpad, gpad, spectral_kernel)
        return (acc + grad, (forward[freq_table], backward[freq_table]))
    init = jnp.zeros((TAPS, F, F), jnp.float32)
    spec_grad, (spec_rows, back_rows) = lax.scan(row_step, init, (jnp.moveaxis(hidden, 2, 0), jnp.moveaxis(cotangent, 2, 0)))
    spec = jnp.moveaxis(spec_rows, 0, 2)
    back = jnp.moveaxis(back_rows, 0, 2)
    restored = (dirty.astype(jnp.float32) + spec.astype(jnp.float32)).astype(jnp.bfloat16)
    back_b = back.reshape(blocks, CH_DEV, F, H, W)

    def backward_block(carry, items):
        kgrad, mgrad = carry
        block, smooth, bgrad, cgrad = items
        smooth32 = smooth.astype(jnp.float32)
        mixed = jnp.einsum('gf,cfhw->cghw', mix32, smooth32)
        dmixed = (bgrad.astype(jnp.float32) * silu_slope(mixed)).astype(jnp.bfloat16)
        dm32 = dmixed.astype(jnp.float32)
        mgrad = mgrad + jnp.einsum('cghw,cfhw->gf', dm32, smooth32)
        dsmooth = jnp.einsum('gf,cghw->cfhw', mix32, dm32).astype(jnp.bfloat16)
        ds32 = dsmooth.astype(jnp.float32)
        dpad = jnp.pad(ds32, ((0, 0), (0, 0), (2, 2), (2, 2)))
        xpad = jnp.pad(block.astype(jnp.float32), ((0, 0), (0, 0), (2, 2), (2, 2)))
        conv = jnp.zeros(block.shape, jnp.float32)
        terms = []
        for i in range(5):
            for j in range(5):
                conv = conv + spatial_kernel[:, i * 5 + j][None, :, None, None] * dpad[:, :, 4 - i:4 - i + H, 4 - j:4 - j + W]
                terms.append(jnp.einsum('cfhw,cfhw->f', ds32, xpad[:, :, i:i + H, j:j + W]))
        kgrad = kgrad + jnp.stack(terms, 1)
        dgrad = (cgrad.astype(jnp.float32) + conv).astype(jnp.bfloat16)
        return ((kgrad, mgrad), dgrad)
    start = (jnp.zeros((F, 25), jnp.float32), jnp.zeros((F, F), jnp.float32))
    (kgrad, mgrad), dgrad_b = lax.scan(backward_block, start, (dirty_b, smooth_b, back_b, cot_b))
    scale = 1.0 / math.sqrt(C * H * W)
    dirty_grad = dgrad_b.reshape(C, F, H, W)
    return (restored, dirty_grad, kgrad * scale, mgrad * scale, spec_grad * scale)
```

```python
import math

import jax
import jax.numpy as jnp
from jax import lax
from jax.sharding import PartitionSpec as P


def padded(block, sides, width):
    for axis, dim in sides:
        count = lax.axis_size(axis)
        forward = [(i, i + 1) for i in range(count - 1)]
        backward = [(target, source) for source, target in forward]
        low = lax.ppermute(
            lax.slice_in_dim(block, block.shape[dim] - width, None, axis=dim), axis, forward
        )
        high = lax.ppermute(lax.slice_in_dim(block, 0, width, axis=dim), axis, backward)
        block = jnp.concatenate([low, block, high], axis=dim)
    return block


def passed_along(block, axis, distance):
    devices = range(lax.axis_size(axis))
    route = [((i - distance) % len(devices), i) for i in devices]
    return lax.ppermute(block, axis, route)


def all_summed(value, axes):
    for axis in axes:
        count = lax.axis_size(axis)
        if count & (count - 1):
            value = lax.psum(value, axis)
            continue
        step = 1
        while step < count:
            value = value + lax.ppermute(value, axis, [(i, i ^ step) for i in range(count)])
            step *= 2
    return value


def silu_slope(value):
    sig = jax.nn.sigmoid(value)
    return sig * (1.0 + value * (1.0 - sig))


def move_down(array):
    return jnp.pad(array, ((1, 0), (0, 0), (0, 0)))[:-1]


def move_up(array):
    return jnp.pad(array, ((0, 1), (0, 0), (0, 0)))[1:]


def local(dirty, cotangent, spatial_kernel, feature_mix, spectral_kernel, freq_table):
    chans, feats, rows, cols = dirty.shape
    taps = spectral_kernel.shape[0]
    half = (taps - 1) // 2
    n_chan = lax.axis_size("chan")
    n_rows = lax.axis_size("tile") * lax.axis_size("sub")
    scale = 1.0 / math.sqrt(chans * n_chan * rows * n_rows * cols)
    pixels = rows * cols
    extended = padded(dirty, ((("tile", "sub"), 2),), 2)
    xpad = jnp.pad(extended, ((0, 0), (0, 0), (0, 0), (2, 2)))
    xpad32 = xpad.astype(jnp.float32)
    total = jnp.zeros(dirty.shape, jnp.float32)
    for i in range(5):
        for j in range(5):
            total = (
                total
                + spatial_kernel[:, i * 5 + j][None, :, None, None]
                * xpad32[:, :, i : i + rows, j : j + cols]
            )
    smooth = total.astype(jnp.bfloat16)
    mixed = jnp.einsum("gf,cfhw->cghw", feature_mix, smooth, preferred_element_type=jnp.float32)
    hidden = jax.nn.silu(mixed).astype(jnp.bfloat16)
    hidden_flat = hidden.reshape(chans, feats, pixels)
    grad_flat = cotangent.reshape(chans, feats, pixels)
    device = lax.axis_index("chan")
    start = device * chans
    own = lax.dynamic_slice_in_dim(freq_table, start, chans) // n_chan
    order = jnp.zeros((chans,), jnp.int32).at[own].set(jnp.arange(chans, dtype=jnp.int32))
    h_sorted = hidden_flat[order]
    g_sorted = grad_flat[order]
    fwd_acc = jnp.einsum(
        "gf,mfp->mgp", spectral_kernel[half], h_sorted, preferred_element_type=jnp.float32
    )
    bwd_acc = jnp.einsum(
        "gf,mgp->mfp", spectral_kernel[half], g_sorted, preferred_element_type=jnp.float32
    )
    grad_taps = [None] * taps
    grad_taps[half] = jnp.einsum(
        "mgp,mfp->gf", g_sorted, h_sorted, preferred_element_type=jnp.float32
    )
    for dist in range(1, half + 1):
        for sign in (-1, 1):
            h_far, g_far = passed_along((h_sorted, g_sorted), "chan", -sign * dist)
            if sign < 0:
                wrapped = device < dist
                h_near = jnp.where(wrapped, move_down(h_far), h_far)
                g_near = jnp.where(wrapped, move_down(g_far), g_far)
            else:
                wrapped = device + dist >= n_chan
                h_near = jnp.where(wrapped, move_up(h_far), h_far)
                g_near = jnp.where(wrapped, move_up(g_far), g_far)
            offset = sign * dist
            fwd_acc = fwd_acc + jnp.einsum(
                "gf,mfp->mgp",
                spectral_kernel[half + offset],
                h_near,
                preferred_element_type=jnp.float32,
            )
            bwd_acc = bwd_acc + jnp.einsum(
                "gf,mgp->mfp",
                spectral_kernel[half - offset],
                g_near,
                preferred_element_type=jnp.float32,
            )
            grad_taps[half + offset] = jnp.einsum(
                "mgp,mfp->gf", g_sorted, h_near, preferred_element_type=jnp.float32
            )
    spec_grad = jnp.stack(grad_taps, 0)
    spec_flat = fwd_acc.astype(jnp.bfloat16)[own]
    back_flat = bwd_acc.astype(jnp.bfloat16)[own]
    spec = spec_flat.reshape(chans, feats, rows, cols)
    back = back_flat.reshape(chans, feats, rows, cols)
    restored = (dirty.astype(jnp.float32) + spec.astype(jnp.float32)).astype(jnp.bfloat16)
    dmixed = (back.astype(jnp.float32) * silu_slope(mixed)).astype(jnp.bfloat16)
    mix_term = jnp.einsum("cghw,cfhw->gf", dmixed, smooth, preferred_element_type=jnp.float32)
    dsmooth = jnp.einsum(
        "gf,cghw->cfhw", feature_mix, dmixed, preferred_element_type=jnp.float32
    ).astype(jnp.bfloat16)
    grad_ext = padded(dsmooth, ((("tile", "sub"), 2),), 2)
    dpad32 = jnp.pad(grad_ext, ((0, 0), (0, 0), (0, 0), (2, 2))).astype(jnp.float32)
    conv = jnp.zeros(dirty.shape, jnp.float32)
    terms = []
    for i in range(5):
        for j in range(5):
            conv = (
                conv
                + spatial_kernel[:, i * 5 + j][None, :, None, None]
                * dpad32[:, :, 4 - i : 4 - i + rows, 4 - j : 4 - j + cols]
            )
            terms.append(
                jnp.einsum(
                    "cfhw,cfhw->f",
                    dsmooth,
                    xpad[:, :, i : i + rows, j : j + cols],
                    preferred_element_type=jnp.float32,
                )
            )
    kernel_term = jnp.stack(terms, 1)
    dirty_grad = (cotangent.astype(jnp.float32) + conv).astype(jnp.bfloat16)
    parts = (kernel_term, mix_term, spec_grad)
    flat = all_summed(jnp.concatenate([part.reshape(-1) for part in parts]), ("sub", "tile", "chan"))
    sizes = [part.size for part in parts]
    kgrad, mgrad, sgrad = (
        piece.reshape(part.shape)
        for piece, part in zip(jnp.split(flat, [sizes[0], sizes[0] + sizes[1]]), parts)
    )
    return (restored, dirty_grad, kgrad * scale, mgrad * scale, sgrad * scale)


def solution(mesh):
    in_specs = (
        P(("grp", "chan"), None, ("tile", "sub"), None),
        P(("grp", "chan"), None, ("tile", "sub"), None),
        P(),
        P(),
        P(),
        P(),
    )
    out_specs = (
        P(("grp", "chan"), None, ("tile", "sub"), None),
        P(("grp", "chan"), None, ("tile", "sub"), None),
        P("grp", None),
        P("grp", None),
        P("grp", None, None),
    )
    return jax.shard_map(local, mesh=mesh, in_specs=in_specs, out_specs=out_specs, check_vma=False)
```

```python
import math

import jax
import jax.numpy as jnp
from jax import lax
from jax.sharding import PartitionSpec as P


def padded(block, sides, width):
    for axis, dim in sides:
        count = lax.axis_size(axis)
        forward = [(i, i + 1) for i in range(count - 1)]
        backward = [(target, source) for source, target in forward]
        low = lax.ppermute(
            lax.slice_in_dim(block, block.shape[dim] - width, None, axis=dim), axis, forward
        )
        high = lax.ppermute(lax.slice_in_dim(block, 0, width, axis=dim), axis, backward)
        block = jnp.concatenate([low, block, high], axis=dim)
    return block


def passed_along(block, axis, distance):
    devices = range(lax.axis_size(axis))
    route = [((i - distance) % len(devices), i) for i in devices]
    return lax.ppermute(block, axis, route)


def all_summed(value, axes):
    for axis in axes:
        count = lax.axis_size(axis)
        if count & (count - 1):
            value = lax.psum(value, axis)
            continue
        step = 1
        while step < count:
            value = value + lax.ppermute(value, axis, [(i, i ^ step) for i in range(count)])
            step *= 2
    return value


def silu_slope(value):
    sig = jax.nn.sigmoid(value)
    return sig * (1.0 + value * (1.0 - sig))


def move_down(array):
    return jnp.pad(array, ((1, 0), (0, 0), (0, 0)))[:-1]


def move_up(array):
    return jnp.pad(array, ((0, 1), (0, 0), (0, 0)))[1:]


def local(dirty, cotangent, spatial_kernel, feature_mix, spectral_kernel, freq_table):
    chans, feats, rows, cols = dirty.shape
    taps = spectral_kernel.shape[0]
    half = (taps - 1) // 2
    n_chan = lax.axis_size("chan")
    n_rows = lax.axis_size("tile") * lax.axis_size("sub")
    scale = 1.0 / math.sqrt(chans * n_chan * rows * n_rows * cols)
    pixels = rows * cols
    extended = padded(dirty, ((("tile", "sub"), 2),), 2)
    xpad = jnp.pad(extended, ((0, 0), (0, 0), (0, 0), (2, 2)))
    xpad32 = xpad.astype(jnp.float32)
    total = jnp.zeros(dirty.shape, jnp.float32)
    for i in range(5):
        for j in range(5):
            total = (
                total
                + spatial_kernel[:, i * 5 + j][None, :, None, None]
                * xpad32[:, :, i : i + rows, j : j + cols]
            )
    smooth = total.astype(jnp.bfloat16)
    mixed = jnp.einsum("gf,cfhw->cghw", feature_mix, smooth, preferred_element_type=jnp.float32)
    hidden = jax.nn.silu(mixed).astype(jnp.bfloat16)
    hidden_flat = hidden.reshape(chans, feats, pixels)
    grad_flat = cotangent.reshape(chans, feats, pixels)
    device = lax.axis_index("chan")
    start = device * chans
    own = lax.dynamic_slice_in_dim(freq_table, start, chans) // n_chan
    order = jnp.zeros((chans,), jnp.int32).at[own].set(jnp.arange(chans, dtype=jnp.int32))
    h_sorted = hidden_flat[order]
    g_sorted = grad_flat[order]
    h_taps = [h_sorted] * taps
    g_taps = [g_sorted] * taps
    for dist in range(1, half + 1):
        for sign in (-1, 1):
            h_far = passed_along(h_sorted, "chan", -sign * dist)
            g_far = passed_along(g_sorted, "chan", -sign * dist)
            if sign < 0:
                wrapped = device < dist
                h_near = jnp.where(wrapped, move_down(h_far), h_far)
                g_near = jnp.where(wrapped, move_down(g_far), g_far)
            else:
                wrapped = device + dist >= n_chan
                h_near = jnp.where(wrapped, move_up(h_far), h_far)
                g_near = jnp.where(wrapped, move_up(g_far), g_far)
            h_taps[half + sign * dist] = h_near
            g_taps[half + sign * dist] = g_near
    h_stack = jnp.stack(h_taps, 1).reshape(chans, taps * feats, pixels)
    g_stack = jnp.stack(g_taps, 1).reshape(chans, taps * feats, pixels)
    fwd_weight = spectral_kernel.transpose(1, 0, 2).reshape(feats, taps * feats)
    bwd_weight = spectral_kernel[::-1].transpose(2, 0, 1).reshape(feats, taps * feats)
    fwd_acc = jnp.einsum("gK,mKp->mgp", fwd_weight, h_stack, preferred_element_type=jnp.float32)
    bwd_acc = jnp.einsum("fK,mKp->mfp", bwd_weight, g_stack, preferred_element_type=jnp.float32)
    spec_grad = jnp.einsum(
        "mKp,mfp->Kf", g_stack, h_sorted, preferred_element_type=jnp.float32
    ).reshape(taps, feats, feats)[::-1]
    spec_flat = fwd_acc.astype(jnp.bfloat16)[own]
    back_flat = bwd_acc.astype(jnp.bfloat16)[own]
    spec = spec_flat.reshape(chans, feats, rows, cols)
    back = back_flat.reshape(chans, feats, rows, cols)
    restored = (dirty.astype(jnp.float32) + spec.astype(jnp.float32)).astype(jnp.bfloat16)
    dmixed = (back.astype(jnp.float32) * silu_slope(mixed)).astype(jnp.bfloat16)
    mix_term = jnp.einsum("cghw,cfhw->gf", dmixed, smooth, preferred_element_type=jnp.float32)
    dsmooth = jnp.einsum(
        "gf,cghw->cfhw", feature_mix, dmixed, preferred_element_type=jnp.float32
    ).astype(jnp.bfloat16)
    grad_ext = padded(dsmooth, ((("tile", "sub"), 2),), 2)
    dpad32 = jnp.pad(grad_ext, ((0, 0), (0, 0), (0, 0), (2, 2))).astype(jnp.float32)
    conv = jnp.zeros(dirty.shape, jnp.float32)
    terms = []
    for i in range(5):
        for j in range(5):
            conv = (
                conv
                + spatial_kernel[:, i * 5 + j][None, :, None, None]
                * dpad32[:, :, 4 - i : 4 - i + rows, 4 - j : 4 - j + cols]
            )
            terms.append(
                jnp.einsum(
                    "cfhw,cfhw->f",
                    dsmooth,
                    xpad[:, :, i : i + rows, j : j + cols],
                    preferred_element_type=jnp.float32,
                )
            )
    kernel_term = jnp.stack(terms, 1)
    dirty_grad = (cotangent.astype(jnp.float32) + conv).astype(jnp.bfloat16)
    parts = (kernel_term, mix_term, spec_grad)
    flat = jnp.concatenate([part.reshape(-1) for part in parts]) * scale
    flat = all_summed(flat, ("sub", "tile", "chan"))
    sizes = [part.size for part in parts]
    kgrad, mgrad, sgrad = (
        piece.reshape(part.shape)
        for piece, part in zip(jnp.split(flat, [sizes[0], sizes[0] + sizes[1]]), parts)
    )
    return (restored, dirty_grad, kgrad, mgrad, sgrad)


def solution(mesh):
    in_specs = (
        P(("grp", "chan"), None, ("tile", "sub"), None),
        P(("grp", "chan"), None, ("tile", "sub"), None),
        P(),
        P(),
        P(),
        P(),
    )
    out_specs = (
        P(("grp", "chan"), None, ("tile", "sub"), None),
        P(("grp", "chan"), None, ("tile", "sub"), None),
        P("grp", None),
        P("grp", None),
        P("grp", None, None),
    )
    return jax.shard_map(local, mesh=mesh, in_specs=in_specs, out_specs=out_specs, check_vma=False)
```

```python
import math

import jax
import jax.numpy as jnp
from jax import lax
from jax.sharding import PartitionSpec as P


def padded(block, sides, width):
    for axis, dim in sides:
        count = lax.axis_size(axis)
        forward = [(i, i + 1) for i in range(count - 1)]
        backward = [(target, source) for source, target in forward]
        low = lax.ppermute(
            lax.slice_in_dim(block, block.shape[dim] - width, None, axis=dim), axis, forward
        )
        high = lax.ppermute(lax.slice_in_dim(block, 0, width, axis=dim), axis, backward)
        block = jnp.concatenate([low, block, high], axis=dim)
    return block


def passed_along(block, axis, distance):
    devices = range(lax.axis_size(axis))
    route = [((i - distance) % len(devices), i) for i in devices]
    return lax.ppermute(block, axis, route)


def all_summed(value, axes, tied=None):
    rounds = []
    for axis in axes:
        count = lax.axis_size(axis)
        if count & (count - 1):
            rounds.append((axis, 0))
        else:
            rounds.extend((axis, 1 << bit) for bit in range(count.bit_length() - 1))
    for index, (axis, step) in enumerate(rounds):
        if tied is not None and index == len(rounds) - 1:
            value, _ = lax.optimization_barrier((value, tied))
        if step == 0:
            value = lax.psum(value, axis)
        else:
            count = lax.axis_size(axis)
            value = value + lax.ppermute(value, axis, [(i, i ^ step) for i in range(count)])
    return value


def silu_slope(value):
    sig = jax.nn.sigmoid(value)
    return sig * (1.0 + value * (1.0 - sig))


def move_down(array):
    return jnp.pad(array, ((1, 0), (0, 0), (0, 0)))[:-1]


def move_up(array):
    return jnp.pad(array, ((0, 1), (0, 0), (0, 0)))[1:]


def local(dirty, cotangent, spatial_kernel, feature_mix, spectral_kernel, freq_table):
    chans, feats, rows, cols = dirty.shape
    taps = spectral_kernel.shape[0]
    half = (taps - 1) // 2
    n_chan = lax.axis_size("chan")
    n_rows = lax.axis_size("tile") * lax.axis_size("sub")
    scale = 1.0 / math.sqrt(chans * n_chan * rows * n_rows * cols)
    pixels = rows * cols
    extended = padded(dirty, ((("tile", "sub"), 2),), 2)
    xpad = jnp.pad(extended, ((0, 0), (0, 0), (0, 0), (2, 2)))
    xpad32 = xpad.astype(jnp.float32)
    total = jnp.zeros(dirty.shape, jnp.float32)
    for i in range(5):
        for j in range(5):
            total = (
                total
                + spatial_kernel[:, i * 5 + j][None, :, None, None]
                * xpad32[:, :, i : i + rows, j : j + cols]
            )
    smooth = total.astype(jnp.bfloat16)
    mixed = jnp.einsum("gf,cfhw->cghw", feature_mix, smooth, preferred_element_type=jnp.float32)
    hidden = jax.nn.silu(mixed).astype(jnp.bfloat16)
    hidden_flat = hidden.reshape(chans, feats, pixels)
    grad_flat = cotangent.reshape(chans, feats, pixels)
    device = lax.axis_index("chan")
    start = device * chans
    own = lax.dynamic_slice_in_dim(freq_table, start, chans) // n_chan
    order = jnp.zeros((chans,), jnp.int32).at[own].set(jnp.arange(chans, dtype=jnp.int32))
    h_sorted = hidden_flat[order]
    g_sorted = grad_flat[order]
    h_taps = [h_sorted] * taps
    h_received = []
    g_received = []
    g_taps = [g_sorted] * taps
    for dist in range(1, half + 1):
        for sign in (-1, 1):
            h_far = passed_along(h_sorted, "chan", -sign * dist)
            h_received.append(h_far)
            g_far = passed_along(g_sorted, "chan", -sign * dist)
            g_received.append(g_far)
    g_received, mixed_late = lax.optimization_barrier((g_received, mixed))
    for index, (dist, sign) in enumerate((d, s) for d in range(1, half + 1) for s in (-1, 1)):
        if sign < 0:
            wrapped = device < dist
            shift = move_down
        else:
            wrapped = device + dist >= n_chan
            shift = move_up
        h_far, g_far = h_received[index], g_received[index]
        h_taps[half + sign * dist] = jnp.where(wrapped, shift(h_far), h_far)
        g_taps[half + sign * dist] = jnp.where(wrapped, shift(g_far), g_far)
    h_stack = jnp.stack(h_taps, 1).reshape(chans, taps * feats, pixels)
    g_stack = jnp.stack(g_taps, 1).reshape(chans, taps * feats, pixels)
    fwd_weight = spectral_kernel.transpose(1, 0, 2).reshape(feats, taps * feats)
    bwd_weight = spectral_kernel[::-1].transpose(2, 0, 1).reshape(feats, taps * feats)
    fwd_acc = jnp.einsum("gK,mKp->mgp", fwd_weight, h_stack, preferred_element_type=jnp.float32)
    bwd_acc = jnp.einsum("fK,mKp->mfp", bwd_weight, g_stack, preferred_element_type=jnp.float32)
    spec_grad = jnp.einsum(
        "mKp,mfp->Kf", g_stack, h_sorted, preferred_element_type=jnp.float32
    ).reshape(taps, feats, feats)[::-1]
    spec_flat = fwd_acc.astype(jnp.bfloat16)[own]
    back_flat = bwd_acc.astype(jnp.bfloat16)[own]
    spec = spec_flat.reshape(chans, feats, rows, cols)
    back = back_flat.reshape(chans, feats, rows, cols)
    restored = (dirty.astype(jnp.float32) + spec.astype(jnp.float32)).astype(jnp.bfloat16)
    dmixed = (back.astype(jnp.float32) * silu_slope(mixed_late)).astype(jnp.bfloat16)
    mix_term = jnp.einsum("cghw,cfhw->gf", dmixed, smooth, preferred_element_type=jnp.float32)
    dsmooth = jnp.einsum(
        "gf,cghw->cfhw", feature_mix, dmixed, preferred_element_type=jnp.float32
    ).astype(jnp.bfloat16)
    grad_ext = padded(dsmooth, ((("tile", "sub"), 2),), 2)
    dpad32 = jnp.pad(grad_ext, ((0, 0), (0, 0), (0, 0), (2, 2))).astype(jnp.float32)
    conv = jnp.zeros(dirty.shape, jnp.float32)
    terms = []
    for i in range(5):
        for j in range(5):
            conv = (
                conv
                + spatial_kernel[:, i * 5 + j][None, :, None, None]
                * dpad32[:, :, 4 - i : 4 - i + rows, 4 - j : 4 - j + cols]
            )
            terms.append(
                jnp.einsum(
                    "cfhw,cfhw->f",
                    dsmooth,
                    xpad[:, :, i : i + rows, j : j + cols],
                    preferred_element_type=jnp.float32,
                )
            )
    kernel_term = jnp.stack(terms, 1)
    dirty_grad = (cotangent.astype(jnp.float32) + conv).astype(jnp.bfloat16)
    parts = (kernel_term, mix_term, spec_grad)
    flat = jnp.concatenate([part.reshape(-1) for part in parts]) * scale
    flat = all_summed(flat, ("sub", "tile", "chan"), tied=h_received)
    sizes = [part.size for part in parts]
    kgrad, mgrad, sgrad = (
        piece.reshape(part.shape)
        for piece, part in zip(jnp.split(flat, [sizes[0], sizes[0] + sizes[1]]), parts)
    )
    return (restored, dirty_grad, kgrad, mgrad, sgrad)


def solution(mesh):
    in_specs = (
        P(("grp", "chan"), None, ("tile", "sub"), None),
        P(("grp", "chan"), None, ("tile", "sub"), None),
        P(),
        P(),
        P(),
        P(),
    )
    out_specs = (
        P(("grp", "chan"), None, ("tile", "sub"), None),
        P(("grp", "chan"), None, ("tile", "sub"), None),
        P("grp", None),
        P("grp", None),
        P("grp", None, None),
    )
    return jax.shard_map(local, mesh=mesh, in_specs=in_specs, out_specs=out_specs, check_vma=False)
```

```python
import math

import jax
import jax.numpy as jnp
from jax import lax
from jax.sharding import PartitionSpec as P


def padded(block, sides, width):
    for axis, dim in sides:
        count = lax.axis_size(axis)
        forward = [(i, i + 1) for i in range(count - 1)]
        backward = [(target, source) for source, target in forward]
        low = lax.ppermute(
            lax.slice_in_dim(block, block.shape[dim] - width, None, axis=dim), axis, forward
        )
        high = lax.ppermute(lax.slice_in_dim(block, 0, width, axis=dim), axis, backward)
        block = jnp.concatenate([low, block, high], axis=dim)
    return block


def passed_along(block, axis, distance):
    devices = range(lax.axis_size(axis))
    route = [((i - distance) % len(devices), i) for i in devices]
    return lax.ppermute(block, axis, route)


def all_summed(value, axes, tied=None):
    rounds = []
    for axis in axes:
        count = lax.axis_size(axis)
        if count & (count - 1):
            rounds.append((axis, 0))
        else:
            rounds.extend((axis, 1 << bit) for bit in range(count.bit_length() - 1))
    for index, (axis, step) in enumerate(rounds):
        if tied is not None and index == [name for name, _ in rounds].index(axes[-1]):
            value, _ = lax.optimization_barrier((value, tied))
        if step == 0:
            value = lax.psum(value, axis)
        else:
            count = lax.axis_size(axis)
            value = value + lax.ppermute(value, axis, [(i, i ^ step) for i in range(count)])
    return value


def silu_slope(value):
    sig = jax.nn.sigmoid(value)
    return sig * (1.0 + value * (1.0 - sig))


def order_of(inverse, source, chans, n_chan):
    return lax.dynamic_index_in_dim(inverse.reshape(chans, n_chan), source, 1, keepdims=False) - source * chans


def move_down(array):
    return jnp.pad(array, ((1, 0), (0, 0), (0, 0)))[:-1]


def move_up(array):
    return jnp.pad(array, ((0, 1), (0, 0), (0, 0)))[1:]


def local(dirty, cotangent, spatial_kernel, feature_mix, spectral_kernel, freq_table):
    chans, feats, rows, cols = dirty.shape
    taps = spectral_kernel.shape[0]
    half = (taps - 1) // 2
    n_chan = lax.axis_size("chan")
    n_rows = lax.axis_size("tile") * lax.axis_size("sub")
    scale = 1.0 / math.sqrt(chans * n_chan * rows * n_rows * cols)
    pixels = rows * cols
    extended = padded(dirty, ((("tile", "sub"), 2),), 2)
    xpad = jnp.pad(extended, ((0, 0), (0, 0), (0, 0), (2, 2)))
    xpad32 = xpad.astype(jnp.float32)
    total = jnp.zeros(dirty.shape, jnp.float32)
    for i in range(5):
        for j in range(5):
            total = (
                total
                + spatial_kernel[:, i * 5 + j][None, :, None, None]
                * xpad32[:, :, i : i + rows, j : j + cols]
            )
    smooth = total.astype(jnp.bfloat16)
    mixed = jnp.einsum("gf,cfhw->cghw", feature_mix, smooth, preferred_element_type=jnp.float32)
    hidden = jax.nn.silu(mixed).astype(jnp.bfloat16)
    hidden_flat = hidden.reshape(chans, feats, pixels)
    grad_flat = cotangent.reshape(chans, feats, pixels)
    device = lax.axis_index("chan")
    start = device * chans
    own = lax.dynamic_slice_in_dim(freq_table, start, chans) // n_chan
    total_chans = freq_table.shape[0]
    inverse = jnp.zeros((total_chans,), jnp.int32).at[freq_table].set(jnp.arange(total_chans, dtype=jnp.int32))
    order = order_of(inverse, device, chans, n_chan)
    h_sorted = hidden_flat[order]
    g_sorted = grad_flat[order]
    h_received = []
    g_received = []
    for dist in range(1, half + 1):
        for sign in (-1, 1):
            g_received.append(passed_along(grad_flat, "chan", -sign * dist))
    g_received, h_sorted, mixed_late = lax.optimization_barrier((g_received, h_sorted, mixed))
    for dist in range(1, half + 1):
        for sign in (-1, 1):
            h_received.append(passed_along(h_sorted, "chan", -sign * dist))
    h_taps = [h_sorted] * taps
    g_taps = [g_sorted] * taps
    for index, (dist, sign) in enumerate((d, s) for d in range(1, half + 1) for s in (-1, 1)):
        if sign < 0:
            wrapped = device < dist
            shift = move_down
        else:
            wrapped = device + dist >= n_chan
            shift = move_up
        source = (device + sign * dist) % n_chan
        h_far = h_received[index]
        g_far = g_received[index][order_of(inverse, source, chans, n_chan)]
        h_taps[half + sign * dist] = jnp.where(wrapped, shift(h_far), h_far)
        g_taps[half + sign * dist] = jnp.where(wrapped, shift(g_far), g_far)
    h_stack = jnp.stack(h_taps, 1).reshape(chans, taps * feats, pixels)
    g_stack = jnp.stack(g_taps, 1).reshape(chans, taps * feats, pixels)
    fwd_weight = spectral_kernel.transpose(1, 0, 2).reshape(feats, taps * feats)
    bwd_weight = spectral_kernel[::-1].transpose(2, 0, 1).reshape(feats, taps * feats)
    fwd_acc = jnp.einsum("gK,mKp->mgp", fwd_weight, h_stack, preferred_element_type=jnp.float32)
    bwd_acc = jnp.einsum("fK,mKp->mfp", bwd_weight, g_stack, preferred_element_type=jnp.float32)
    spec_grad = jnp.einsum(
        "mKp,mfp->Kf", g_stack, h_sorted, preferred_element_type=jnp.float32
    ).reshape(taps, feats, feats)[::-1]
    spec_flat = fwd_acc.astype(jnp.bfloat16)[own]
    back_flat = bwd_acc.astype(jnp.bfloat16)[own]
    spec = spec_flat.reshape(chans, feats, rows, cols)
    back = back_flat.reshape(chans, feats, rows, cols)
    restored = (dirty.astype(jnp.float32) + spec.astype(jnp.float32)).astype(jnp.bfloat16)
    dmixed = (back.astype(jnp.float32) * silu_slope(mixed_late)).astype(jnp.bfloat16)
    mix_term = jnp.einsum("cghw,cfhw->gf", dmixed, smooth, preferred_element_type=jnp.float32)
    dsmooth = jnp.einsum(
        "gf,cghw->cfhw", feature_mix, dmixed, preferred_element_type=jnp.float32
    ).astype(jnp.bfloat16)
    grad_ext = padded(dsmooth, ((("tile", "sub"), 2),), 2)
    dpad32 = jnp.pad(grad_ext, ((0, 0), (0, 0), (0, 0), (2, 2))).astype(jnp.float32)
    conv = jnp.zeros(dirty.shape, jnp.float32)
    terms = []
    for i in range(5):
        for j in range(5):
            conv = (
                conv
                + spatial_kernel[:, i * 5 + j][None, :, None, None]
                * dpad32[:, :, 4 - i : 4 - i + rows, 4 - j : 4 - j + cols]
            )
            terms.append(
                jnp.einsum(
                    "cfhw,cfhw->f",
                    dsmooth,
                    xpad[:, :, i : i + rows, j : j + cols],
                    preferred_element_type=jnp.float32,
                )
            )
    kernel_term = jnp.stack(terms, 1)
    dirty_grad = (cotangent.astype(jnp.float32) + conv).astype(jnp.bfloat16)
    parts = (kernel_term, mix_term, spec_grad)
    flat = jnp.concatenate([part.reshape(-1) for part in parts]) * scale
    flat = all_summed(flat, ("sub", "tile", "chan"), tied=h_received)
    sizes = [part.size for part in parts]
    kgrad, mgrad, sgrad = (
        piece.reshape(part.shape)
        for piece, part in zip(jnp.split(flat, [sizes[0], sizes[0] + sizes[1]]), parts)
    )
    return (restored, dirty_grad, kgrad, mgrad, sgrad)


def solution(mesh):
    in_specs = (
        P(("grp", "chan"), None, ("tile", "sub"), None),
        P(("grp", "chan"), None, ("tile", "sub"), None),
        P(),
        P(),
        P(),
        P(),
    )
    out_specs = (
        P(("grp", "chan"), None, ("tile", "sub"), None),
        P(("grp", "chan"), None, ("tile", "sub"), None),
        P("grp", None),
        P("grp", None),
        P("grp", None, None),
    )
    return jax.shard_map(local, mesh=mesh, in_specs=in_specs, out_specs=out_specs, check_vma=False)
```

```python
import math

import jax
import jax.numpy as jnp
from jax import lax
from jax.sharding import PartitionSpec as P


def padded(block, sides, width):
    for axis, dim in sides:
        count = lax.axis_size(axis)
        forward = [(i, i + 1) for i in range(count - 1)]
        backward = [(target, source) for source, target in forward]
        low = lax.ppermute(
            lax.slice_in_dim(block, block.shape[dim] - width, None, axis=dim), axis, forward
        )
        high = lax.ppermute(lax.slice_in_dim(block, 0, width, axis=dim), axis, backward)
        block = jnp.concatenate([low, block, high], axis=dim)
    return block


def passed_along(block, axis, distance):
    devices = range(lax.axis_size(axis))
    route = [((i - distance) % len(devices), i) for i in devices]
    return lax.ppermute(block, axis, route)


def all_summed(value, axes):
    for axis in axes:
        count = lax.axis_size(axis)
        if count & (count - 1):
            value = lax.psum(value, axis)
            continue
        step = 1
        while step < count:
            value = value + lax.ppermute(value, axis, [(i, i ^ step) for i in range(count)])
            step *= 2
    return value


def exchanged(pieces, axis):
    count = lax.axis_size(axis)
    if count > 8:
        return lax.all_to_all(pieces, axis, 0, 0), jnp.arange(count)
    device = lax.axis_index(axis)
    held = [lax.dynamic_index_in_dim(pieces, device, 0, keepdims=False)]
    for step in range(1, count):
        piece = lax.dynamic_index_in_dim(pieces, (device + step) % count, 0, keepdims=False)
        held.append(lax.ppermute(piece, axis, [(i, (i + step) % count) for i in range(count)]))
    return jnp.stack(held, 0), (device - jnp.arange(count)) % count


def silu_slope(value):
    sig = jax.nn.sigmoid(value)
    return sig * (1.0 + value * (1.0 - sig))


def move_down(array):
    return jnp.pad(array, ((1, 0), (0, 0), (0, 0)))[:-1]


def move_up(array):
    return jnp.pad(array, ((0, 1), (0, 0), (0, 0)))[1:]


def local(dirty, cotangent, spatial_kernel, feature_mix, spectral_kernel, freq_table):
    chans, feats, rows, cols = dirty.shape
    taps = spectral_kernel.shape[0]
    half = (taps - 1) // 2
    n_chan = lax.axis_size("chan")
    n_rows = lax.axis_size("tile") * lax.axis_size("sub")
    scale = 1.0 / math.sqrt(chans * n_chan * rows * n_rows * cols)
    pixels = rows * cols
    extended = padded(dirty, ((("tile", "sub"), 2),), 2)
    xpad = jnp.pad(extended, ((0, 0), (0, 0), (0, 0), (2, 2)))
    xpad32 = xpad.astype(jnp.float32)
    total = jnp.zeros(dirty.shape, jnp.float32)
    for i in range(5):
        for j in range(5):
            total = (
                total
                + spatial_kernel[:, i * 5 + j][None, :, None, None]
                * xpad32[:, :, i : i + rows, j : j + cols]
            )
    smooth = total.astype(jnp.bfloat16)
    mixed = jnp.einsum("gf,cfhw->cghw", feature_mix, smooth, preferred_element_type=jnp.float32)
    hidden = jax.nn.silu(mixed).astype(jnp.bfloat16)
    total_chans = freq_table.shape[0]
    chunk = pixels // n_chan
    inverse = jnp.zeros((total_chans,), jnp.int32).at[freq_table].set(
        jnp.arange(total_chans, dtype=jnp.int32)
    )

    def to_freq_major(block):
        pieces = block.reshape(chans, feats, n_chan, chunk).transpose(2, 0, 1, 3)
        held, slot = exchanged(pieces, "chan")
        rows_of = slot[inverse // chans] * chans + inverse % chans
        return held.reshape(n_chan * chans, feats, chunk)[rows_of]

    def to_pixel_major(values):
        pieces = values.astype(jnp.bfloat16)[freq_table.reshape(n_chan, chans)]
        held, slot = exchanged(pieces, "chan")
        return held[slot].transpose(1, 2, 0, 3).reshape(chans, feats, rows, cols)

    def stacked(values):
        ends = jnp.pad(values, ((half, half), (0, 0), (0, 0)))
        return jnp.stack([ends[k : k + total_chans] for k in range(taps)], 1).reshape(
            total_chans, taps * feats, chunk
        )

    g_freq = to_freq_major(cotangent)
    g_stack = stacked(g_freq)
    bwd_weight = spectral_kernel[::-1].transpose(2, 0, 1).reshape(feats, taps * feats)
    bwd_acc = jnp.einsum("fK,qKp->qfp", bwd_weight, g_stack, preferred_element_type=jnp.float32)
    back = to_pixel_major(bwd_acc)
    h_freq = to_freq_major(hidden)
    h_stack = stacked(h_freq)
    fwd_weight = spectral_kernel.transpose(1, 0, 2).reshape(feats, taps * feats)
    fwd_acc = jnp.einsum("gK,qKp->qgp", fwd_weight, h_stack, preferred_element_type=jnp.float32)
    spec = to_pixel_major(fwd_acc)
    spec_grad = jnp.einsum(
        "qKp,qfp->Kf", g_stack, h_freq, preferred_element_type=jnp.float32
    ).reshape(taps, feats, feats)[::-1]
    restored = (dirty.astype(jnp.float32) + spec.astype(jnp.float32)).astype(jnp.bfloat16)
    dmixed = (back.astype(jnp.float32) * silu_slope(mixed)).astype(jnp.bfloat16)
    mix_term = jnp.einsum("cghw,cfhw->gf", dmixed, smooth, preferred_element_type=jnp.float32)
    dsmooth = jnp.einsum(
        "gf,cghw->cfhw", feature_mix, dmixed, preferred_element_type=jnp.float32
    ).astype(jnp.bfloat16)
    grad_ext = padded(dsmooth, ((("tile", "sub"), 2),), 2)
    dpad32 = jnp.pad(grad_ext, ((0, 0), (0, 0), (0, 0), (2, 2))).astype(jnp.float32)
    conv = jnp.zeros(dirty.shape, jnp.float32)
    terms = []
    for i in range(5):
        for j in range(5):
            conv = (
                conv
                + spatial_kernel[:, i * 5 + j][None, :, None, None]
                * dpad32[:, :, 4 - i : 4 - i + rows, 4 - j : 4 - j + cols]
            )
            terms.append(
                jnp.einsum(
                    "cfhw,cfhw->f",
                    dsmooth,
                    xpad[:, :, i : i + rows, j : j + cols],
                    preferred_element_type=jnp.float32,
                )
            )
    kernel_term = jnp.stack(terms, 1)
    dirty_grad = (cotangent.astype(jnp.float32) + conv).astype(jnp.bfloat16)
    parts = (kernel_term, mix_term, spec_grad)
    flat = jnp.concatenate([part.reshape(-1) for part in parts]) * scale
    flat = all_summed(flat, ("sub", "tile", "chan"))
    sizes = [part.size for part in parts]
    kgrad, mgrad, sgrad = (
        piece.reshape(part.shape)
        for piece, part in zip(jnp.split(flat, [sizes[0], sizes[0] + sizes[1]]), parts)
    )
    return (restored, dirty_grad, kgrad, mgrad, sgrad)


def solution(mesh):
    in_specs = (
        P(("grp", "chan"), None, ("tile", "sub"), None),
        P(("grp", "chan"), None, ("tile", "sub"), None),
        P(),
        P(),
        P(),
        P(),
    )
    out_specs = (
        P(("grp", "chan"), None, ("tile", "sub"), None),
        P(("grp", "chan"), None, ("tile", "sub"), None),
        P("grp", None),
        P("grp", None),
        P("grp", None, None),
    )
    return jax.shard_map(local, mesh=mesh, in_specs=in_specs, out_specs=out_specs, check_vma=False)
```

```python
import math

import jax
import jax.numpy as jnp
from jax import lax
from jax.sharding import PartitionSpec as P


def padded(block, sides, width):
    for axis, dim in sides:
        count = lax.axis_size(axis)
        forward = [(i, i + 1) for i in range(count - 1)]
        backward = [(target, source) for source, target in forward]
        low = lax.ppermute(
            lax.slice_in_dim(block, block.shape[dim] - width, None, axis=dim), axis, forward
        )
        high = lax.ppermute(lax.slice_in_dim(block, 0, width, axis=dim), axis, backward)
        block = jnp.concatenate([low, block, high], axis=dim)
    return block


def passed_along(block, axis, distance):
    devices = range(lax.axis_size(axis))
    route = [((i - distance) % len(devices), i) for i in devices]
    return lax.ppermute(block, axis, route)


def all_summed(value, axes, tied=None):
    if tied is not None:
        value, _ = lax.optimization_barrier((value, tied))
    for axis in axes:
        count = lax.axis_size(axis)
        if count & (count - 1):
            value = lax.psum(value, axis)
            continue
        step = 1
        while step < count:
            value = value + lax.ppermute(value, axis, [(i, i ^ step) for i in range(count)])
            step *= 2
    return value


def silu_slope(value):
    sig = jax.nn.sigmoid(value)
    return sig * (1.0 + value * (1.0 - sig))


def move_down(array):
    return jnp.pad(array, ((1, 0), (0, 0), (0, 0)))[:-1]


def move_up(array):
    return jnp.pad(array, ((0, 1), (0, 0), (0, 0)))[1:]


def local(dirty, cotangent, spatial_kernel, feature_mix, spectral_kernel, freq_table):
    chans, feats, rows, cols = dirty.shape
    taps = spectral_kernel.shape[0]
    half = (taps - 1) // 2
    n_chan = lax.axis_size("chan")
    n_rows = lax.axis_size("tile") * lax.axis_size("sub")
    scale = 1.0 / math.sqrt(chans * n_chan * rows * n_rows * cols)
    pixels = rows * cols
    extended = padded(dirty, ((("tile", "sub"), 2),), 2)
    xpad = jnp.pad(extended, ((0, 0), (0, 0), (0, 0), (2, 2)))
    xpad32 = xpad.astype(jnp.float32)
    total = jnp.zeros(dirty.shape, jnp.float32)
    for i in range(5):
        for j in range(5):
            total = (
                total
                + spatial_kernel[:, i * 5 + j][None, :, None, None]
                * xpad32[:, :, i : i + rows, j : j + cols]
            )
    smooth = total.astype(jnp.bfloat16)
    mixed = jnp.einsum("gf,cfhw->cghw", feature_mix, smooth, preferred_element_type=jnp.float32)
    hidden = jax.nn.silu(mixed).astype(jnp.bfloat16)
    hidden_flat = hidden.reshape(chans, feats, pixels)
    grad_flat = cotangent.reshape(chans, feats, pixels)
    device = lax.axis_index("chan")
    start = device * chans
    own = lax.dynamic_slice_in_dim(freq_table, start, chans) // n_chan
    order = jnp.zeros((chans,), jnp.int32).at[own].set(jnp.arange(chans, dtype=jnp.int32))
    h_sorted = hidden_flat[order]
    g_sorted = grad_flat[order]
    h_taps = [h_sorted] * taps
    h_received = []
    g_taps = [g_sorted] * taps
    for dist in range(1, half + 1):
        for sign in (-1, 1):
            h_far = passed_along(h_sorted, "chan", -sign * dist)
            h_received.append(h_far)
            g_far = passed_along(g_sorted, "chan", -sign * dist)
            if sign < 0:
                wrapped = device < dist
                h_near = jnp.where(wrapped, move_down(h_far), h_far)
                g_near = jnp.where(wrapped, move_down(g_far), g_far)
            else:
                wrapped = device + dist >= n_chan
                h_near = jnp.where(wrapped, move_up(h_far), h_far)
                g_near = jnp.where(wrapped, move_up(g_far), g_far)
            h_taps[half + sign * dist] = h_near
            g_taps[half + sign * dist] = g_near
    h_stack = jnp.stack(h_taps, 1).reshape(chans, taps * feats, pixels)
    g_stack = jnp.stack(g_taps, 1).reshape(chans, taps * feats, pixels)
    fwd_weight = spectral_kernel.transpose(1, 0, 2).reshape(feats, taps * feats)
    bwd_weight = spectral_kernel[::-1].transpose(2, 0, 1).reshape(feats, taps * feats)
    fwd_acc = jnp.einsum("gK,mKp->mgp", fwd_weight, h_stack, preferred_element_type=jnp.float32)
    bwd_acc = jnp.einsum("fK,mKp->mfp", bwd_weight, g_stack, preferred_element_type=jnp.float32)
    spec_grad = jnp.einsum(
        "mKp,mfp->Kf", g_stack, h_sorted, preferred_element_type=jnp.float32
    ).reshape(taps, feats, feats)[::-1]
    spec_flat = fwd_acc.astype(jnp.bfloat16)[own]
    back_flat = bwd_acc.astype(jnp.bfloat16)[own]
    spec = spec_flat.reshape(chans, feats, rows, cols)
    back = back_flat.reshape(chans, feats, rows, cols)
    restored = (dirty.astype(jnp.float32) + spec.astype(jnp.float32)).astype(jnp.bfloat16)
    dmixed = (back.astype(jnp.float32) * silu_slope(mixed)).astype(jnp.bfloat16)
    mix_term = jnp.einsum("cghw,cfhw->gf", dmixed, smooth, preferred_element_type=jnp.float32)
    dsmooth = jnp.einsum(
        "gf,cghw->cfhw", feature_mix, dmixed, preferred_element_type=jnp.float32
    ).astype(jnp.bfloat16)
    grad_ext = padded(dsmooth, ((("tile", "sub"), 2),), 2)
    dpad32 = jnp.pad(grad_ext, ((0, 0), (0, 0), (0, 0), (2, 2))).astype(jnp.float32)
    conv = jnp.zeros(dirty.shape, jnp.float32)
    terms = []
    for i in range(5):
        for j in range(5):
            conv = (
                conv
                + spatial_kernel[:, i * 5 + j][None, :, None, None]
                * dpad32[:, :, 4 - i : 4 - i + rows, 4 - j : 4 - j + cols]
            )
            terms.append(
                jnp.einsum(
                    "cfhw,cfhw->f",
                    dsmooth,
                    xpad[:, :, i : i + rows, j : j + cols],
                    preferred_element_type=jnp.float32,
                )
            )
    kernel_term = jnp.stack(terms, 1)
    dirty_grad = (cotangent.astype(jnp.float32) + conv).astype(jnp.bfloat16)
    parts = (kernel_term, mix_term, spec_grad)
    flat = jnp.concatenate([part.reshape(-1) for part in parts]) * scale
    flat = all_summed(flat, ("sub", "tile", "chan"), tied=h_received)
    sizes = [part.size for part in parts]
    kgrad, mgrad, sgrad = (
        piece.reshape(part.shape)
        for piece, part in zip(jnp.split(flat, [sizes[0], sizes[0] + sizes[1]]), parts)
    )
    return (restored, dirty_grad, kgrad, mgrad, sgrad)


def solution(mesh):
    in_specs = (
        P(("grp", "chan"), None, ("tile", "sub"), None),
        P(("grp", "chan"), None, ("tile", "sub"), None),
        P(),
        P(),
        P(),
        P(),
    )
    out_specs = (
        P(("grp", "chan"), None, ("tile", "sub"), None),
        P(("grp", "chan"), None, ("tile", "sub"), None),
        P("grp", None),
        P("grp", None),
        P("grp", None, None),
    )
    return jax.shard_map(local, mesh=mesh, in_specs=in_specs, out_specs=out_specs, check_vma=False)
```

```python
import math

import jax
import jax.numpy as jnp
from jax import lax
from jax.sharding import PartitionSpec as P


def padded(block, sides, width):
    for axis, dim in sides:
        count = lax.axis_size(axis)
        forward = [(i, i + 1) for i in range(count - 1)]
        backward = [(target, source) for source, target in forward]
        low = lax.ppermute(
            lax.slice_in_dim(block, block.shape[dim] - width, None, axis=dim), axis, forward
        )
        high = lax.ppermute(lax.slice_in_dim(block, 0, width, axis=dim), axis, backward)
        block = jnp.concatenate([low, block, high], axis=dim)
    return block


def passed_along(block, axis, distance):
    devices = range(lax.axis_size(axis))
    route = [((i - distance) % len(devices), i) for i in devices]
    return lax.ppermute(block, axis, route)


def all_summed(value, axes, tied=None, tie_at=0):
    done = 0
    for axis in axes:
        count = lax.axis_size(axis)
        if count & (count - 1):
            value = lax.psum(value, axis)
            continue
        step = 1
        while step < count:
            if tied is not None and done == tie_at:
                value, _ = lax.optimization_barrier((value, tied))
            value = value + lax.ppermute(value, axis, [(i, i ^ step) for i in range(count)])
            step *= 2
            done += 1
    return value


def silu_slope(value):
    sig = jax.nn.sigmoid(value)
    return sig * (1.0 + value * (1.0 - sig))


def move_down(array):
    return jnp.pad(array, ((1, 0), (0, 0), (0, 0)))[:-1]


def move_up(array):
    return jnp.pad(array, ((0, 1), (0, 0), (0, 0)))[1:]


def local(dirty, cotangent, spatial_kernel, feature_mix, spectral_kernel, freq_table):
    chans, feats, rows, cols = dirty.shape
    taps = spectral_kernel.shape[0]
    half = (taps - 1) // 2
    n_chan = lax.axis_size("chan")
    n_rows = lax.axis_size("tile") * lax.axis_size("sub")
    scale = 1.0 / math.sqrt(chans * n_chan * rows * n_rows * cols)
    pixels = rows * cols
    extended = padded(dirty, ((("tile", "sub"), 2),), 2)
    xpad = jnp.pad(extended, ((0, 0), (0, 0), (0, 0), (2, 2)))
    xpad32 = xpad.astype(jnp.float32)
    total = jnp.zeros(dirty.shape, jnp.float32)
    for i in range(5):
        for j in range(5):
            total = (
                total
                + spatial_kernel[:, i * 5 + j][None, :, None, None]
                * xpad32[:, :, i : i + rows, j : j + cols]
            )
    smooth = total.astype(jnp.bfloat16)
    mixed = jnp.einsum("gf,cfhw->cghw", feature_mix, smooth, preferred_element_type=jnp.float32)
    hidden = jax.nn.silu(mixed).astype(jnp.bfloat16)
    hidden_flat = hidden.reshape(chans, feats, pixels)
    grad_flat = cotangent.reshape(chans, feats, pixels)
    device = lax.axis_index("chan")
    start = device * chans
    own = lax.dynamic_slice_in_dim(freq_table, start, chans) // n_chan
    order = jnp.zeros((chans,), jnp.int32).at[own].set(jnp.arange(chans, dtype=jnp.int32))
    h_sorted = hidden_flat[order]
    g_sorted = grad_flat[order]
    h_taps = [h_sorted] * taps
    h_received = []
    g_taps = [g_sorted] * taps
    for dist in range(1, half + 1):
        for sign in (-1, 1):
            h_far = passed_along(h_sorted, "chan", -sign * dist)
            h_received.append(h_far)
            g_far = passed_along(g_sorted, "chan", -sign * dist)
            if sign < 0:
                wrapped = device < dist
                h_near = jnp.where(wrapped, move_down(h_far), h_far)
                g_near = jnp.where(wrapped, move_down(g_far), g_far)
            else:
                wrapped = device + dist >= n_chan
                h_near = jnp.where(wrapped, move_up(h_far), h_far)
                g_near = jnp.where(wrapped, move_up(g_far), g_far)
            h_taps[half + sign * dist] = h_near
            g_taps[half + sign * dist] = g_near
    h_stack = jnp.stack(h_taps, 1).reshape(chans, taps * feats, pixels)
    g_stack = jnp.stack(g_taps, 1).reshape(chans, taps * feats, pixels)
    fwd_weight = spectral_kernel.transpose(1, 0, 2).reshape(feats, taps * feats)
    bwd_weight = spectral_kernel[::-1].transpose(2, 0, 1).reshape(feats, taps * feats)
    fwd_acc = jnp.einsum("gK,mKp->mgp", fwd_weight, h_stack, preferred_element_type=jnp.float32)
    bwd_acc = jnp.einsum("fK,mKp->mfp", bwd_weight, g_stack, preferred_element_type=jnp.float32)
    spec_grad = jnp.einsum(
        "mKp,mfp->Kf", g_stack, h_sorted, preferred_element_type=jnp.float32
    ).reshape(taps, feats, feats)[::-1]
    spec_flat = fwd_acc.astype(jnp.bfloat16)[own]
    back_flat = bwd_acc.astype(jnp.bfloat16)[own]
    spec = spec_flat.reshape(chans, feats, rows, cols)
    back = back_flat.reshape(chans, feats, rows, cols)
    restored = (dirty.astype(jnp.float32) + spec.astype(jnp.float32)).astype(jnp.bfloat16)
    dmixed = (back.astype(jnp.float32) * silu_slope(mixed)).astype(jnp.bfloat16)
    mix_term = jnp.einsum("cghw,cfhw->gf", dmixed, smooth, preferred_element_type=jnp.float32)
    dsmooth = jnp.einsum(
        "gf,cghw->cfhw", feature_mix, dmixed, preferred_element_type=jnp.float32
    ).astype(jnp.bfloat16)
    grad_ext = padded(dsmooth, ((("tile", "sub"), 2),), 2)
    dpad32 = jnp.pad(grad_ext, ((0, 0), (0, 0), (0, 0), (2, 2))).astype(jnp.float32)
    conv = jnp.zeros(dirty.shape, jnp.float32)
    terms = []
    for i in range(5):
        for j in range(5):
            conv = (
                conv
                + spatial_kernel[:, i * 5 + j][None, :, None, None]
                * dpad32[:, :, 4 - i : 4 - i + rows, 4 - j : 4 - j + cols]
            )
            terms.append(
                jnp.einsum(
                    "cfhw,cfhw->f",
                    dsmooth,
                    xpad[:, :, i : i + rows, j : j + cols],
                    preferred_element_type=jnp.float32,
                )
            )
    kernel_term = jnp.stack(terms, 1)
    dirty_grad = (cotangent.astype(jnp.float32) + conv).astype(jnp.bfloat16)
    parts = (kernel_term, mix_term, spec_grad)
    flat = jnp.concatenate([part.reshape(-1) for part in parts]) * scale
    flat = all_summed(flat, ("sub", "tile", "chan"), tied=h_received, tie_at=3)
    sizes = [part.size for part in parts]
    kgrad, mgrad, sgrad = (
        piece.reshape(part.shape)
        for piece, part in zip(jnp.split(flat, [sizes[0], sizes[0] + sizes[1]]), parts)
    )
    return (restored, dirty_grad, kgrad, mgrad, sgrad)


def solution(mesh):
    in_specs = (
        P(("grp", "chan"), None, ("tile", "sub"), None),
        P(("grp", "chan"), None, ("tile", "sub"), None),
        P(),
        P(),
        P(),
        P(),
    )
    out_specs = (
        P(("grp", "chan"), None, ("tile", "sub"), None),
        P(("grp", "chan"), None, ("tile", "sub"), None),
        P("grp", None),
        P("grp", None),
        P("grp", None, None),
    )
    return jax.shard_map(local, mesh=mesh, in_specs=in_specs, out_specs=out_specs, check_vma=False)
```

```python
import math

import jax
import jax.numpy as jnp
from jax import lax
from jax.sharding import PartitionSpec as P


def padded(block, sides, width):
    for axis, dim in sides:
        count = lax.axis_size(axis)
        forward = [(i, i + 1) for i in range(count - 1)]
        backward = [(target, source) for source, target in forward]
        low = lax.ppermute(
            lax.slice_in_dim(block, block.shape[dim] - width, None, axis=dim), axis, forward
        )
        high = lax.ppermute(lax.slice_in_dim(block, 0, width, axis=dim), axis, backward)
        block = jnp.concatenate([low, block, high], axis=dim)
    return block


def passed_along(block, axis, distance):
    devices = range(lax.axis_size(axis))
    route = [((i - distance) % len(devices), i) for i in devices]
    return lax.ppermute(block, axis, route)


def all_summed(value, axes, tied=None, tie_at=0):
    done = 0
    for axis in axes:
        count = lax.axis_size(axis)
        if count & (count - 1):
            value = lax.psum(value, axis)
            continue
        step = 1
        while step < count:
            if tied is not None and done == tie_at:
                value, _ = lax.optimization_barrier((value, tied))
            value = value + lax.ppermute(value, axis, [(i, i ^ step) for i in range(count)])
            step *= 2
            done += 1
    return value


def silu_slope(value):
    sig = jax.nn.sigmoid(value)
    return sig * (1.0 + value * (1.0 - sig))


def move_down(array):
    return jnp.pad(array, ((1, 0), (0, 0), (0, 0)))[:-1]


def move_up(array):
    return jnp.pad(array, ((0, 1), (0, 0), (0, 0)))[1:]


def local(dirty, cotangent, spatial_kernel, feature_mix, spectral_kernel, freq_table):
    chans, feats, rows, cols = dirty.shape
    taps = spectral_kernel.shape[0]
    half = (taps - 1) // 2
    n_chan = lax.axis_size("chan")
    n_rows = lax.axis_size("tile") * lax.axis_size("sub")
    scale = 1.0 / math.sqrt(chans * n_chan * rows * n_rows * cols)
    pixels = rows * cols
    extended = padded(dirty, ((("tile", "sub"), 2),), 2)
    xpad = jnp.pad(extended, ((0, 0), (0, 0), (0, 0), (2, 2)))
    xpad32 = xpad.astype(jnp.float32)
    total = jnp.zeros(dirty.shape, jnp.float32)
    for i in range(5):
        for j in range(5):
            total = (
                total
                + spatial_kernel[:, i * 5 + j][None, :, None, None]
                * xpad32[:, :, i : i + rows, j : j + cols]
            )
    smooth = total.astype(jnp.bfloat16)
    mixed = jnp.einsum("gf,cfhw->cghw", feature_mix, smooth, preferred_element_type=jnp.float32)
    hidden = jax.nn.silu(mixed).astype(jnp.bfloat16)
    hidden_flat = hidden.reshape(chans, feats, pixels)
    grad_flat = cotangent.reshape(chans, feats, pixels)
    device = lax.axis_index("chan")
    start = device * chans
    own = lax.dynamic_slice_in_dim(freq_table, start, chans) // n_chan
    order = jnp.zeros((chans,), jnp.int32).at[own].set(jnp.arange(chans, dtype=jnp.int32))
    h_sorted = hidden_flat[order]
    g_sorted = grad_flat[order]
    h_taps = [h_sorted] * taps
    h_received = []
    g_taps = [g_sorted] * taps
    for dist in range(1, half + 1):
        for sign in (-1, 1):
            h_far = passed_along(h_sorted, "chan", -sign * dist)
            h_received.append(h_far)
            g_far = passed_along(g_sorted, "chan", -sign * dist)
            if sign < 0:
                wrapped = device < dist
                h_near = jnp.where(wrapped, move_down(h_far), h_far)
                g_near = jnp.where(wrapped, move_down(g_far), g_far)
            else:
                wrapped = device + dist >= n_chan
                h_near = jnp.where(wrapped, move_up(h_far), h_far)
                g_near = jnp.where(wrapped, move_up(g_far), g_far)
            h_taps[half + sign * dist] = h_near
            g_taps[half + sign * dist] = g_near
    h_stack = jnp.stack(h_taps, 1).reshape(chans, taps * feats, pixels)
    g_stack = jnp.stack(g_taps, 1).reshape(chans, taps * feats, pixels)
    fwd_weight = spectral_kernel.transpose(1, 0, 2).reshape(feats, taps * feats)
    bwd_weight = spectral_kernel[::-1].transpose(2, 0, 1).reshape(feats, taps * feats)
    fwd_acc = jnp.einsum("gK,mKp->mgp", fwd_weight, h_stack, preferred_element_type=jnp.float32)
    bwd_acc = jnp.einsum("fK,mKp->mfp", bwd_weight, g_stack, preferred_element_type=jnp.float32)
    spec_grad = jnp.einsum(
        "mKp,mfp->Kf", g_stack, h_sorted, preferred_element_type=jnp.float32
    ).reshape(taps, feats, feats)[::-1]
    spec_flat = fwd_acc.astype(jnp.bfloat16)[own]
    back_flat = bwd_acc.astype(jnp.bfloat16)[own]
    spec = spec_flat.reshape(chans, feats, rows, cols)
    back = back_flat.reshape(chans, feats, rows, cols)
    restored = (dirty.astype(jnp.float32) + spec.astype(jnp.float32)).astype(jnp.bfloat16)
    dmixed = (back.astype(jnp.float32) * silu_slope(mixed)).astype(jnp.bfloat16)
    mix_term = jnp.einsum("cghw,cfhw->gf", dmixed, smooth, preferred_element_type=jnp.float32)
    dsmooth = jnp.einsum(
        "gf,cghw->cfhw", feature_mix, dmixed, preferred_element_type=jnp.float32
    ).astype(jnp.bfloat16)
    grad_ext = padded(dsmooth, ((("tile", "sub"), 2),), 2)
    dpad32 = jnp.pad(grad_ext, ((0, 0), (0, 0), (0, 0), (2, 2))).astype(jnp.float32)
    conv = jnp.zeros(dirty.shape, jnp.float32)
    terms = []
    for i in range(5):
        for j in range(5):
            conv = (
                conv
                + spatial_kernel[:, i * 5 + j][None, :, None, None]
                * dpad32[:, :, 4 - i : 4 - i + rows, 4 - j : 4 - j + cols]
            )
            terms.append(
                jnp.einsum(
                    "cfhw,cfhw->f",
                    dsmooth,
                    xpad[:, :, i : i + rows, j : j + cols],
                    preferred_element_type=jnp.float32,
                )
            )
    kernel_term = jnp.stack(terms, 1)
    dirty_grad = (cotangent.astype(jnp.float32) + conv).astype(jnp.bfloat16)
    parts = (kernel_term, mix_term, spec_grad)
    flat = jnp.concatenate([part.reshape(-1) for part in parts]) * scale
    flat = all_summed(flat, ("sub", "tile", "chan"), tied=h_received, tie_at=2)
    sizes = [part.size for part in parts]
    kgrad, mgrad, sgrad = (
        piece.reshape(part.shape)
        for piece, part in zip(jnp.split(flat, [sizes[0], sizes[0] + sizes[1]]), parts)
    )
    return (restored, dirty_grad, kgrad, mgrad, sgrad)


def solution(mesh):
    in_specs = (
        P(("grp", "chan"), None, ("tile", "sub"), None),
        P(("grp", "chan"), None, ("tile", "sub"), None),
        P(),
        P(),
        P(),
        P(),
    )
    out_specs = (
        P(("grp", "chan"), None, ("tile", "sub"), None),
        P(("grp", "chan"), None, ("tile", "sub"), None),
        P("grp", None),
        P("grp", None),
        P("grp", None, None),
    )
    return jax.shard_map(local, mesh=mesh, in_specs=in_specs, out_specs=out_specs, check_vma=False)
```

```python
import math

import jax
import jax.numpy as jnp
from jax import lax
from jax.sharding import PartitionSpec as P


def padded(block, sides, width):
    for axis, dim in sides:
        count = lax.axis_size(axis)
        forward = [(i, i + 1) for i in range(count - 1)]
        backward = [(target, source) for source, target in forward]
        low = lax.ppermute(
            lax.slice_in_dim(block, block.shape[dim] - width, None, axis=dim), axis, forward
        )
        high = lax.ppermute(lax.slice_in_dim(block, 0, width, axis=dim), axis, backward)
        block = jnp.concatenate([low, block, high], axis=dim)
    return block


def passed_along(block, axis, distance):
    devices = range(lax.axis_size(axis))
    route = [((i - distance) % len(devices), i) for i in devices]
    return lax.ppermute(block, axis, route)


def all_summed(value, axes, tied=None, tie_at=0):
    done = 0
    for axis in axes:
        count = lax.axis_size(axis)
        if count & (count - 1):
            value = lax.psum(value, axis)
            continue
        step = 1
        while step < count:
            if tied is not None and done == tie_at:
                value, _ = lax.optimization_barrier((value, tied))
            value = value + lax.ppermute(value, axis, [(i, i ^ step) for i in range(count)])
            step *= 2
            done += 1
    return value


def silu_slope(value):
    sig = jax.nn.sigmoid(value)
    return sig * (1.0 + value * (1.0 - sig))


def order_of(inverse, source, chans, n_chan):
    table = inverse.reshape(chans, n_chan)
    return lax.dynamic_index_in_dim(table, source, 1, keepdims=False) - source * chans


def move_down(array):
    return jnp.pad(array, ((1, 0), (0, 0), (0, 0)))[:-1]


def move_up(array):
    return jnp.pad(array, ((0, 1), (0, 0), (0, 0)))[1:]


def local(dirty, cotangent, spatial_kernel, feature_mix, spectral_kernel, freq_table):
    chans, feats, rows, cols = dirty.shape
    taps = spectral_kernel.shape[0]
    half = (taps - 1) // 2
    n_chan = lax.axis_size("chan")
    n_rows = lax.axis_size("tile") * lax.axis_size("sub")
    scale = 1.0 / math.sqrt(chans * n_chan * rows * n_rows * cols)
    pixels = rows * cols
    extended = padded(dirty, ((("tile", "sub"), 2),), 2)
    xpad = jnp.pad(extended, ((0, 0), (0, 0), (0, 0), (2, 2)))
    xpad32 = xpad.astype(jnp.float32)
    total = jnp.zeros(dirty.shape, jnp.float32)
    for i in range(5):
        for j in range(5):
            total = (
                total
                + spatial_kernel[:, i * 5 + j][None, :, None, None]
                * xpad32[:, :, i : i + rows, j : j + cols]
            )
    smooth = total.astype(jnp.bfloat16)
    mixed = jnp.einsum("gf,cfhw->cghw", feature_mix, smooth, preferred_element_type=jnp.float32)
    hidden = jax.nn.silu(mixed).astype(jnp.bfloat16)
    hidden_flat = hidden.reshape(chans, feats, pixels)
    grad_flat = cotangent.reshape(chans, feats, pixels)
    device = lax.axis_index("chan")
    start = device * chans
    own = lax.dynamic_slice_in_dim(freq_table, start, chans) // n_chan
    total_chans = freq_table.shape[0]
    inverse = jnp.zeros((total_chans,), jnp.int32).at[freq_table].set(
        jnp.arange(total_chans, dtype=jnp.int32)
    )
    order = order_of(inverse, device, chans, n_chan)
    h_sorted = hidden_flat[order]
    g_sorted = grad_flat[order]
    h_taps = [h_sorted] * taps
    g_taps = [g_sorted] * taps
    offsets = [(dist, sign) for dist in range(1, half + 1) for sign in (-1, 1)]
    h_received = [passed_along(h_sorted, "chan", -sign * dist) for dist, sign in offsets]
    g_received = [passed_along(grad_flat, "chan", -sign * dist) for dist, sign in offsets]
    g_received, _ = lax.optimization_barrier((g_received, h_received))
    for (dist, sign), h_far, g_far in zip(offsets, h_received, g_received):
        g_far = g_far[order_of(inverse, (device + sign * dist) % n_chan, chans, n_chan)]
        if sign < 0:
            wrapped = device < dist
            shift = move_down
        else:
            wrapped = device + dist >= n_chan
            shift = move_up
        h_taps[half + sign * dist] = jnp.where(wrapped, shift(h_far), h_far)
        g_taps[half + sign * dist] = jnp.where(wrapped, shift(g_far), g_far)
    h_stack = jnp.stack(h_taps, 1).reshape(chans, taps * feats, pixels)
    g_stack = jnp.stack(g_taps, 1).reshape(chans, taps * feats, pixels)
    fwd_weight = spectral_kernel.transpose(1, 0, 2).reshape(feats, taps * feats)
    bwd_weight = spectral_kernel[::-1].transpose(2, 0, 1).reshape(feats, taps * feats)
    fwd_acc = jnp.einsum("gK,mKp->mgp", fwd_weight, h_stack, preferred_element_type=jnp.float32)
    bwd_acc = jnp.einsum("fK,mKp->mfp", bwd_weight, g_stack, preferred_element_type=jnp.float32)
    spec_grad = jnp.einsum(
        "mKp,mfp->Kf", g_stack, h_sorted, preferred_element_type=jnp.float32
    ).reshape(taps, feats, feats)[::-1]
    spec_flat = fwd_acc.astype(jnp.bfloat16)[own]
    back_flat = bwd_acc.astype(jnp.bfloat16)[own]
    spec = spec_flat.reshape(chans, feats, rows, cols)
    back = back_flat.reshape(chans, feats, rows, cols)
    restored = (dirty.astype(jnp.float32) + spec.astype(jnp.float32)).astype(jnp.bfloat16)
    dmixed = (back.astype(jnp.float32) * silu_slope(mixed)).astype(jnp.bfloat16)
    mix_term = jnp.einsum("cghw,cfhw->gf", dmixed, smooth, preferred_element_type=jnp.float32)
    dsmooth = jnp.einsum(
        "gf,cghw->cfhw", feature_mix, dmixed, preferred_element_type=jnp.float32
    ).astype(jnp.bfloat16)
    grad_ext = padded(dsmooth, ((("tile", "sub"), 2),), 2)
    dpad32 = jnp.pad(grad_ext, ((0, 0), (0, 0), (0, 0), (2, 2))).astype(jnp.float32)
    conv = jnp.zeros(dirty.shape, jnp.float32)
    terms = []
    for i in range(5):
        for j in range(5):
            conv = (
                conv
                + spatial_kernel[:, i * 5 + j][None, :, None, None]
                * dpad32[:, :, 4 - i : 4 - i + rows, 4 - j : 4 - j + cols]
            )
            terms.append(
                jnp.einsum(
                    "cfhw,cfhw->f",
                    dsmooth,
                    xpad[:, :, i : i + rows, j : j + cols],
                    preferred_element_type=jnp.float32,
                )
            )
    kernel_term = jnp.stack(terms, 1)
    dirty_grad = (cotangent.astype(jnp.float32) + conv).astype(jnp.bfloat16)
    parts = (kernel_term, mix_term, spec_grad)
    flat = jnp.concatenate([part.reshape(-1) for part in parts]) * scale
    flat = all_summed(flat, ("sub", "tile", "chan"), tied=None)
    sizes = [part.size for part in parts]
    kgrad, mgrad, sgrad = (
        piece.reshape(part.shape)
        for piece, part in zip(jnp.split(flat, [sizes[0], sizes[0] + sizes[1]]), parts)
    )
    return (restored, dirty_grad, kgrad, mgrad, sgrad)


def solution(mesh):
    in_specs = (
        P(("grp", "chan"), None, ("tile", "sub"), None),
        P(("grp", "chan"), None, ("tile", "sub"), None),
        P(),
        P(),
        P(),
        P(),
    )
    out_specs = (
        P(("grp", "chan"), None, ("tile", "sub"), None),
        P(("grp", "chan"), None, ("tile", "sub"), None),
        P("grp", None),
        P("grp", None),
        P("grp", None, None),
    )
    return jax.shard_map(local, mesh=mesh, in_specs=in_specs, out_specs=out_specs, check_vma=False)
```

```python
import math

import jax
import jax.numpy as jnp
from jax import lax
from jax.sharding import PartitionSpec as P


def padded(block, sides, width):
    for axis, dim in sides:
        count = lax.axis_size(axis)
        forward = [(i, i + 1) for i in range(count - 1)]
        backward = [(target, source) for source, target in forward]
        low = lax.ppermute(
            lax.slice_in_dim(block, block.shape[dim] - width, None, axis=dim), axis, forward
        )
        high = lax.ppermute(lax.slice_in_dim(block, 0, width, axis=dim), axis, backward)
        block = jnp.concatenate([low, block, high], axis=dim)
    return block


def passed_along(block, axis, distance):
    devices = range(lax.axis_size(axis))
    route = [((i - distance) % len(devices), i) for i in devices]
    return lax.ppermute(block, axis, route)


def all_summed(value, axes, ties=()):
    done = 0
    for axis in axes:
        count = lax.axis_size(axis)
        if count & (count - 1):
            value = lax.psum(value, axis)
            continue
        step = 1
        while step < count:
            for position, tied in ties:
                if done == position:
                    value, _ = lax.optimization_barrier((value, tied))
            value = value + lax.ppermute(value, axis, [(i, i ^ step) for i in range(count)])
            step *= 2
            done += 1
    return value


def silu_slope(value):
    sig = jax.nn.sigmoid(value)
    return sig * (1.0 + value * (1.0 - sig))


def move_down(array):
    return jnp.pad(array, ((1, 0), (0, 0), (0, 0)))[:-1]


def move_up(array):
    return jnp.pad(array, ((0, 1), (0, 0), (0, 0)))[1:]


def local(dirty, cotangent, spatial_kernel, feature_mix, spectral_kernel, freq_table):
    chans, feats, rows, cols = dirty.shape
    taps = spectral_kernel.shape[0]
    half = (taps - 1) // 2
    n_chan = lax.axis_size("chan")
    n_rows = lax.axis_size("tile") * lax.axis_size("sub")
    scale = 1.0 / math.sqrt(chans * n_chan * rows * n_rows * cols)
    pixels = rows * cols
    extended = padded(dirty, ((("tile", "sub"), 2),), 2)
    xpad = jnp.pad(extended, ((0, 0), (0, 0), (0, 0), (2, 2)))
    xpad32 = xpad.astype(jnp.float32)
    total = jnp.zeros(dirty.shape, jnp.float32)
    for i in range(5):
        for j in range(5):
            total = (
                total
                + spatial_kernel[:, i * 5 + j][None, :, None, None]
                * xpad32[:, :, i : i + rows, j : j + cols]
            )
    smooth = total.astype(jnp.bfloat16)
    mixed = jnp.einsum("gf,cfhw->cghw", feature_mix, smooth, preferred_element_type=jnp.float32)
    hidden = jax.nn.silu(mixed).astype(jnp.bfloat16)
    hidden_flat = hidden.reshape(chans, feats, pixels)
    grad_flat = cotangent.reshape(chans, feats, pixels)
    device = lax.axis_index("chan")
    start = device * chans
    own = lax.dynamic_slice_in_dim(freq_table, start, chans) // n_chan
    order = jnp.zeros((chans,), jnp.int32).at[own].set(jnp.arange(chans, dtype=jnp.int32))
    h_sorted = hidden_flat[order]
    g_sorted = grad_flat[order]
    h_taps = [h_sorted] * taps
    h_received = []
    g_taps = [g_sorted] * taps
    for dist in range(1, half + 1):
        for sign in (-1, 1):
            h_far = passed_along(h_sorted, "chan", -sign * dist)
            h_received.append(h_far)
            g_far = passed_along(g_sorted, "chan", -sign * dist)
            if sign < 0:
                wrapped = device < dist
                h_near = jnp.where(wrapped, move_down(h_far), h_far)
                g_near = jnp.where(wrapped, move_down(g_far), g_far)
            else:
                wrapped = device + dist >= n_chan
                h_near = jnp.where(wrapped, move_up(h_far), h_far)
                g_near = jnp.where(wrapped, move_up(g_far), g_far)
            h_taps[half + sign * dist] = h_near
            g_taps[half + sign * dist] = g_near
    h_stack = jnp.stack(h_taps, 1).reshape(chans, taps * feats, pixels)
    g_stack = jnp.stack(g_taps, 1).reshape(chans, taps * feats, pixels)
    fwd_weight = spectral_kernel.transpose(1, 0, 2).reshape(feats, taps * feats)
    bwd_weight = spectral_kernel[::-1].transpose(2, 0, 1).reshape(feats, taps * feats)
    fwd_acc = jnp.einsum("gK,mKp->mgp", fwd_weight, h_stack, preferred_element_type=jnp.float32)
    bwd_acc = jnp.einsum("fK,mKp->mfp", bwd_weight, g_stack, preferred_element_type=jnp.float32)
    spec_grad = jnp.einsum(
        "mKp,mfp->Kf", g_stack, h_sorted, preferred_element_type=jnp.float32
    ).reshape(taps, feats, feats)[::-1]
    spec_flat = fwd_acc.astype(jnp.bfloat16)[own]
    back_flat = bwd_acc.astype(jnp.bfloat16)[own]
    spec = spec_flat.reshape(chans, feats, rows, cols)
    back = back_flat.reshape(chans, feats, rows, cols)
    restored = (dirty.astype(jnp.float32) + spec.astype(jnp.float32)).astype(jnp.bfloat16)
    dmixed = (back.astype(jnp.float32) * silu_slope(mixed)).astype(jnp.bfloat16)
    mix_term = jnp.einsum("cghw,cfhw->gf", dmixed, smooth, preferred_element_type=jnp.float32)
    dsmooth = jnp.einsum(
        "gf,cghw->cfhw", feature_mix, dmixed, preferred_element_type=jnp.float32
    ).astype(jnp.bfloat16)
    grad_ext = padded(dsmooth, ((("tile", "sub"), 2),), 2)
    dpad32 = jnp.pad(grad_ext, ((0, 0), (0, 0), (0, 0), (2, 2))).astype(jnp.float32)
    conv = jnp.zeros(dirty.shape, jnp.float32)
    terms = []
    for i in range(5):
        for j in range(5):
            conv = (
                conv
                + spatial_kernel[:, i * 5 + j][None, :, None, None]
                * dpad32[:, :, 4 - i : 4 - i + rows, 4 - j : 4 - j + cols]
            )
            terms.append(
                jnp.einsum(
                    "cfhw,cfhw->f",
                    dsmooth,
                    xpad[:, :, i : i + rows, j : j + cols],
                    preferred_element_type=jnp.float32,
                )
            )
    kernel_term = jnp.stack(terms, 1)
    dirty_grad = (cotangent.astype(jnp.float32) + conv).astype(jnp.bfloat16)
    parts = (kernel_term, mix_term, spec_grad)
    flat = jnp.concatenate([part.reshape(-1) for part in parts]) * scale
    flat = all_summed(flat, ("sub", "tile", "chan"), ties=((2, grad_ext), (3, h_received)))
    sizes = [part.size for part in parts]
    kgrad, mgrad, sgrad = (
        piece.reshape(part.shape)
        for piece, part in zip(jnp.split(flat, [sizes[0], sizes[0] + sizes[1]]), parts)
    )
    return (restored, dirty_grad, kgrad, mgrad, sgrad)


def solution(mesh):
    in_specs = (
        P(("grp", "chan"), None, ("tile", "sub"), None),
        P(("grp", "chan"), None, ("tile", "sub"), None),
        P(),
        P(),
        P(),
        P(),
    )
    out_specs = (
        P(("grp", "chan"), None, ("tile", "sub"), None),
        P(("grp", "chan"), None, ("tile", "sub"), None),
        P("grp", None),
        P("grp", None),
        P("grp", None, None),
    )
    return jax.shard_map(local, mesh=mesh, in_specs=in_specs, out_specs=out_specs, check_vma=False)
```

```python
import math

import jax
import jax.numpy as jnp
from jax import lax
from jax.sharding import PartitionSpec as P


def padded(block, sides, width):
    for axis, dim in sides:
        count = lax.axis_size(axis)
        forward = [(i, i + 1) for i in range(count - 1)]
        backward = [(target, source) for source, target in forward]
        low = lax.ppermute(
            lax.slice_in_dim(block, block.shape[dim] - width, None, axis=dim), axis, forward
        )
        high = lax.ppermute(lax.slice_in_dim(block, 0, width, axis=dim), axis, backward)
        block = jnp.concatenate([low, block, high], axis=dim)
    return block


def passed_along(block, axis, distance):
    devices = range(lax.axis_size(axis))
    route = [((i - distance) % len(devices), i) for i in devices]
    return lax.ppermute(block, axis, route)


def all_summed(value, axes, pieces, tied=None, tie_at=0):
    rounds = []
    for axis in axes:
        count = lax.axis_size(axis)
        if count & (count - 1):
            rounds.append((axis, 0))
        else:
            rounds.extend((axis, 1 << bit) for bit in range(count.bit_length() - 1))
    received = None
    for done, (axis, step) in enumerate(rounds):
        if received is not None:
            value = value + received
            received = None
        if tied is not None and done == tie_at:
            value, _ = lax.optimization_barrier((value, tied))
        if step == 0:
            value = lax.psum(value, axis)
        else:
            count = lax.axis_size(axis)
            received = lax.ppermute(value, axis, [(i, i ^ step) for i in range(count)])
    if received is not None:
        return tuple(
            (value[lo : lo + size] + received[lo : lo + size]).reshape(shape)
            for lo, size, shape in pieces
        )
    return tuple(value[lo : lo + size].reshape(shape) for lo, size, shape in pieces)


def silu_slope(value):
    sig = jax.nn.sigmoid(value)
    return sig * (1.0 + value * (1.0 - sig))


def move_down(array):
    return jnp.pad(array, ((1, 0), (0, 0), (0, 0)))[:-1]


def move_up(array):
    return jnp.pad(array, ((0, 1), (0, 0), (0, 0)))[1:]


def local(dirty, cotangent, spatial_kernel, feature_mix, spectral_kernel, freq_table):
    chans, feats, rows, cols = dirty.shape
    taps = spectral_kernel.shape[0]
    half = (taps - 1) // 2
    n_chan = lax.axis_size("chan")
    n_rows = lax.axis_size("tile") * lax.axis_size("sub")
    scale = 1.0 / math.sqrt(chans * n_chan * rows * n_rows * cols)
    pixels = rows * cols
    extended = padded(dirty, ((("tile", "sub"), 2),), 2)
    xpad = jnp.pad(extended, ((0, 0), (0, 0), (0, 0), (2, 2)))
    xpad32 = xpad.astype(jnp.float32)
    total = jnp.zeros(dirty.shape, jnp.float32)
    for i in range(5):
        for j in range(5):
            total = (
                total
                + spatial_kernel[:, i * 5 + j][None, :, None, None]
                * xpad32[:, :, i : i + rows, j : j + cols]
            )
    smooth = total.astype(jnp.bfloat16)
    mixed = jnp.einsum("gf,cfhw->cghw", feature_mix, smooth, preferred_element_type=jnp.float32)
    hidden = jax.nn.silu(mixed).astype(jnp.bfloat16)
    hidden_flat = hidden.reshape(chans, feats, pixels)
    grad_flat = cotangent.reshape(chans, feats, pixels)
    device = lax.axis_index("chan")
    start = device * chans
    own = lax.dynamic_slice_in_dim(freq_table, start, chans) // n_chan
    order = jnp.zeros((chans,), jnp.int32).at[own].set(jnp.arange(chans, dtype=jnp.int32))
    h_sorted = hidden_flat[order]
    g_sorted = grad_flat[order]
    h_taps = [h_sorted] * taps
    h_received = []
    g_taps = [g_sorted] * taps
    for dist in range(1, half + 1):
        for sign in (-1, 1):
            h_far = passed_along(h_sorted, "chan", -sign * dist)
            h_received.append(h_far)
            g_far = passed_along(g_sorted, "chan", -sign * dist)
            if sign < 0:
                wrapped = device < dist
                h_near = jnp.where(wrapped, move_down(h_far), h_far)
                g_near = jnp.where(wrapped, move_down(g_far), g_far)
            else:
                wrapped = device + dist >= n_chan
                h_near = jnp.where(wrapped, move_up(h_far), h_far)
                g_near = jnp.where(wrapped, move_up(g_far), g_far)
            h_taps[half + sign * dist] = h_near
            g_taps[half + sign * dist] = g_near
    h_stack = jnp.stack(h_taps, 1).reshape(chans, taps * feats, pixels)
    g_stack = jnp.stack(g_taps, 1).reshape(chans, taps * feats, pixels)
    fwd_weight = spectral_kernel.transpose(1, 0, 2).reshape(feats, taps * feats)
    bwd_weight = spectral_kernel[::-1].transpose(2, 0, 1).reshape(feats, taps * feats)
    fwd_acc = jnp.einsum("gK,mKp->mgp", fwd_weight, h_stack, preferred_element_type=jnp.float32)
    bwd_acc = jnp.einsum("fK,mKp->mfp", bwd_weight, g_stack, preferred_element_type=jnp.float32)
    spec_grad = jnp.einsum(
        "mKp,mfp->Kf", g_stack, h_sorted, preferred_element_type=jnp.float32
    ).reshape(taps, feats, feats)[::-1]
    spec_flat = fwd_acc.astype(jnp.bfloat16)[own]
    back_flat = bwd_acc.astype(jnp.bfloat16)[own]
    spec = spec_flat.reshape(chans, feats, rows, cols)
    back = back_flat.reshape(chans, feats, rows, cols)
    restored = (dirty.astype(jnp.float32) + spec.astype(jnp.float32)).astype(jnp.bfloat16)
    dmixed = (back.astype(jnp.float32) * silu_slope(mixed)).astype(jnp.bfloat16)
    mix_term = jnp.einsum("cghw,cfhw->gf", dmixed, smooth, preferred_element_type=jnp.float32)
    dsmooth = jnp.einsum(
        "gf,cghw->cfhw", feature_mix, dmixed, preferred_element_type=jnp.float32
    ).astype(jnp.bfloat16)
    grad_ext = padded(dsmooth, ((("tile", "sub"), 2),), 2)
    dpad32 = jnp.pad(grad_ext, ((0, 0), (0, 0), (0, 0), (2, 2))).astype(jnp.float32)
    conv = jnp.zeros(dirty.shape, jnp.float32)
    terms = []
    for i in range(5):
        for j in range(5):
            conv = (
                conv
                + spatial_kernel[:, i * 5 + j][None, :, None, None]
                * dpad32[:, :, 4 - i : 4 - i + rows, 4 - j : 4 - j + cols]
            )
            terms.append(
                jnp.einsum(
                    "cfhw,cfhw->f",
                    dsmooth,
                    xpad[:, :, i : i + rows, j : j + cols],
                    preferred_element_type=jnp.float32,
                )
            )
    kernel_term = jnp.stack(terms, 1)
    dirty_grad = (cotangent.astype(jnp.float32) + conv).astype(jnp.bfloat16)
    parts = (kernel_term, mix_term, spec_grad)
    flat = jnp.concatenate([part.reshape(-1) for part in parts]) * scale
    starts = [0, parts[0].size, parts[0].size + parts[1].size]
    pieces = [(lo, part.size, part.shape) for lo, part in zip(starts, parts)]
    kgrad, mgrad, sgrad = all_summed(
        flat, ("sub", "tile", "chan"), pieces, tied=h_received, tie_at=3
    )
    return (restored, dirty_grad, kgrad, mgrad, sgrad)


def solution(mesh):
    in_specs = (
        P(("grp", "chan"), None, ("tile", "sub"), None),
        P(("grp", "chan"), None, ("tile", "sub"), None),
        P(),
        P(),
        P(),
        P(),
    )
    out_specs = (
        P(("grp", "chan"), None, ("tile", "sub"), None),
        P(("grp", "chan"), None, ("tile", "sub"), None),
        P("grp", None),
        P("grp", None),
        P("grp", None, None),
    )
    return jax.shard_map(local, mesh=mesh, in_specs=in_specs, out_specs=out_specs, check_vma=False)
```

```python
import math

import jax
import jax.numpy as jnp
from jax import lax
from jax.sharding import PartitionSpec as P


def padded(block, sides, width):
    for axis, dim in sides:
        count = lax.axis_size(axis)
        forward = [(i, i + 1) for i in range(count - 1)]
        backward = [(target, source) for source, target in forward]
        low = lax.ppermute(
            lax.slice_in_dim(block, block.shape[dim] - width, None, axis=dim), axis, forward
        )
        high = lax.ppermute(lax.slice_in_dim(block, 0, width, axis=dim), axis, backward)
        block = jnp.concatenate([low, block, high], axis=dim)
    return block


def passed_along(block, axis, distance):
    devices = range(lax.axis_size(axis))
    route = [((i - distance) % len(devices), i) for i in devices]
    return lax.ppermute(block, axis, route)


def all_summed(value, axes, tied=None, tie_at=0):
    done = 0
    for axis in axes:
        count = lax.axis_size(axis)
        if count & (count - 1):
            value = lax.psum(value, axis)
            continue
        step = 1
        while step < count:
            if tied is not None and done == tie_at:
                value, _ = lax.optimization_barrier((value, tied))
            value = value + lax.ppermute(value, axis, [(i, i ^ step) for i in range(count)])
            step *= 2
            done += 1
    return value


def silu_slope(value):
    sig = jax.nn.sigmoid(value)
    return sig * (1.0 + value * (1.0 - sig))


def move_down(array):
    return jnp.pad(array, ((1, 0), (0, 0), (0, 0)))[:-1]


def move_up(array):
    return jnp.pad(array, ((0, 1), (0, 0), (0, 0)))[1:]


def local(dirty, cotangent, spatial_kernel, feature_mix, spectral_kernel, freq_table):
    chans, feats, rows, cols = dirty.shape
    taps = spectral_kernel.shape[0]
    half = (taps - 1) // 2
    n_chan = lax.axis_size("chan")
    n_rows = lax.axis_size("tile") * lax.axis_size("sub")
    scale = 1.0 / math.sqrt(chans * n_chan * rows * n_rows * cols)
    pixels = rows * cols
    extended = padded(dirty, ((("tile", "sub"), 2),), 2)
    xpad = jnp.pad(extended, ((0, 0), (0, 0), (0, 0), (2, 2)))
    xpad32 = xpad.astype(jnp.float32)
    total = jnp.zeros(dirty.shape, jnp.float32)
    for i in range(5):
        for j in range(5):
            total = (
                total
                + spatial_kernel[:, i * 5 + j][None, :, None, None]
                * xpad32[:, :, i : i + rows, j : j + cols]
            )
    smooth = total.astype(jnp.bfloat16)
    mixed = jnp.einsum("gf,cfhw->cghw", feature_mix, smooth, preferred_element_type=jnp.float32)
    hidden = jax.nn.silu(mixed).astype(jnp.bfloat16)
    hidden_flat = hidden.reshape(chans, feats, pixels)
    grad_flat = cotangent.reshape(chans, feats, pixels)
    device = lax.axis_index("chan")
    start = device * chans
    own = lax.dynamic_slice_in_dim(freq_table, start, chans) // n_chan
    order = jnp.zeros((chans,), jnp.int32).at[own].set(jnp.arange(chans, dtype=jnp.int32))
    h_sorted = hidden_flat[order]
    g_sorted = grad_flat[order]
    h_taps = [h_sorted] * taps
    h_received = []
    g_taps = [g_sorted] * taps
    for dist in range(1, half + 1):
        for sign in (-1, 1):
            h_far = passed_along(h_sorted, "chan", -sign * dist)
            h_received.append(h_far)
            g_far, _ = lax.optimization_barrier((passed_along(g_sorted, "chan", -sign * dist), mixed))
            if sign < 0:
                wrapped = device < dist
                h_near = jnp.where(wrapped, move_down(h_far), h_far)
                g_near = jnp.where(wrapped, move_down(g_far), g_far)
            else:
                wrapped = device + dist >= n_chan
                h_near = jnp.where(wrapped, move_up(h_far), h_far)
                g_near = jnp.where(wrapped, move_up(g_far), g_far)
            h_taps[half + sign * dist] = h_near
            g_taps[half + sign * dist] = g_near
    h_stack = jnp.stack(h_taps, 1).reshape(chans, taps * feats, pixels)
    g_stack = jnp.stack(g_taps, 1).reshape(chans, taps * feats, pixels)
    fwd_weight = spectral_kernel.transpose(1, 0, 2).reshape(feats, taps * feats)
    bwd_weight = spectral_kernel[::-1].transpose(2, 0, 1).reshape(feats, taps * feats)
    fwd_acc = jnp.einsum("gK,mKp->mgp", fwd_weight, h_stack, preferred_element_type=jnp.float32)
    bwd_acc = jnp.einsum("fK,mKp->mfp", bwd_weight, g_stack, preferred_element_type=jnp.float32)
    spec_grad = jnp.einsum(
        "mKp,mfp->Kf", g_stack, h_sorted, preferred_element_type=jnp.float32
    ).reshape(taps, feats, feats)[::-1]
    spec_flat = fwd_acc.astype(jnp.bfloat16)[own]
    back_flat = bwd_acc.astype(jnp.bfloat16)[own]
    spec = spec_flat.reshape(chans, feats, rows, cols)
    back = back_flat.reshape(chans, feats, rows, cols)
    restored = (dirty.astype(jnp.float32) + spec.astype(jnp.float32)).astype(jnp.bfloat16)
    dmixed = (back.astype(jnp.float32) * silu_slope(mixed)).astype(jnp.bfloat16)
    mix_term = jnp.einsum("cghw,cfhw->gf", dmixed, smooth, preferred_element_type=jnp.float32)
    dsmooth = jnp.einsum(
        "gf,cghw->cfhw", feature_mix, dmixed, preferred_element_type=jnp.float32
    ).astype(jnp.bfloat16)
    grad_ext = padded(dsmooth, ((("tile", "sub"), 2),), 2)
    dpad32 = jnp.pad(grad_ext, ((0, 0), (0, 0), (0, 0), (2, 2))).astype(jnp.float32)
    conv = jnp.zeros(dirty.shape, jnp.float32)
    terms = []
    for i in range(5):
        for j in range(5):
            conv = (
                conv
                + spatial_kernel[:, i * 5 + j][None, :, None, None]
                * dpad32[:, :, 4 - i : 4 - i + rows, 4 - j : 4 - j + cols]
            )
            terms.append(
                jnp.einsum(
                    "cfhw,cfhw->f",
                    dsmooth,
                    xpad[:, :, i : i + rows, j : j + cols],
                    preferred_element_type=jnp.float32,
                )
            )
    kernel_term = jnp.stack(terms, 1)
    dirty_grad = (cotangent.astype(jnp.float32) + conv).astype(jnp.bfloat16)
    parts = (kernel_term, mix_term, spec_grad)
    flat = jnp.concatenate([part.reshape(-1) for part in parts]) * scale
    flat = all_summed(flat, ("sub", "tile", "chan"), tied=h_received, tie_at=1)
    sizes = [part.size for part in parts]
    kgrad, mgrad, sgrad = (
        piece.reshape(part.shape)
        for piece, part in zip(jnp.split(flat, [sizes[0], sizes[0] + sizes[1]]), parts)
    )
    return (restored, dirty_grad, kgrad, mgrad, sgrad)


def solution(mesh):
    in_specs = (
        P(("grp", "chan"), None, ("tile", "sub"), None),
        P(("grp", "chan"), None, ("tile", "sub"), None),
        P(),
        P(),
        P(),
        P(),
    )
    out_specs = (
        P(("grp", "chan"), None, ("tile", "sub"), None),
        P(("grp", "chan"), None, ("tile", "sub"), None),
        P("grp", None),
        P("grp", None),
        P("grp", None, None),
    )
    return jax.shard_map(local, mesh=mesh, in_specs=in_specs, out_specs=out_specs, check_vma=False)
```

```python
import math

import jax
import jax.numpy as jnp
from jax import lax
from jax.sharding import PartitionSpec as P


def padded(block, sides, width):
    for axis, dim in sides:
        count = lax.axis_size(axis)
        forward = [(i, i + 1) for i in range(count - 1)]
        backward = [(target, source) for source, target in forward]
        low = lax.ppermute(
            lax.slice_in_dim(block, block.shape[dim] - width, None, axis=dim), axis, forward
        )
        high = lax.ppermute(lax.slice_in_dim(block, 0, width, axis=dim), axis, backward)
        block = jnp.concatenate([low, block, high], axis=dim)
    return block


def passed_along(block, axis, distance):
    devices = range(lax.axis_size(axis))
    route = [((i - distance) % len(devices), i) for i in devices]
    return lax.ppermute(block, axis, route)


def all_summed(value, axes, tied=None, tie_at=0):
    done = 0
    for axis in axes:
        count = lax.axis_size(axis)
        if count & (count - 1):
            value = lax.psum(value, axis)
            continue
        step = 1
        while step < count:
            if tied is not None and done == tie_at:
                value, _ = lax.optimization_barrier((value, tied))
            value = value + lax.ppermute(value, axis, [(i, i ^ step) for i in range(count)])
            step *= 2
            done += 1
    return value


def silu_slope(value):
    sig = jax.nn.sigmoid(value)
    return sig * (1.0 + value * (1.0 - sig))


def move_down(array):
    return jnp.pad(array, ((1, 0), (0, 0), (0, 0)))[:-1]


def move_up(array):
    return jnp.pad(array, ((0, 1), (0, 0), (0, 0)))[1:]


def local(dirty, cotangent, spatial_kernel, feature_mix, spectral_kernel, freq_table):
    chans, feats, rows, cols = dirty.shape
    taps = spectral_kernel.shape[0]
    half = (taps - 1) // 2
    n_chan = lax.axis_size("chan")
    n_rows = lax.axis_size("tile") * lax.axis_size("sub")
    scale = 1.0 / math.sqrt(chans * n_chan * rows * n_rows * cols)
    pixels = rows * cols
    extended = padded(dirty, ((("tile", "sub"), 2),), 2)
    xpad = jnp.pad(extended, ((0, 0), (0, 0), (0, 0), (2, 2)))
    xpad32 = xpad.astype(jnp.float32)
    total = jnp.zeros(dirty.shape, jnp.float32)
    for i in range(5):
        for j in range(5):
            total = (
                total
                + spatial_kernel[:, i * 5 + j][None, :, None, None]
                * xpad32[:, :, i : i + rows, j : j + cols]
            )
    smooth = total.astype(jnp.bfloat16)
    mixed = jnp.einsum("gf,cfhw->cghw", feature_mix, smooth, preferred_element_type=jnp.float32)
    hidden = jax.nn.silu(mixed).astype(jnp.bfloat16)
    hidden_flat = hidden.reshape(chans, feats, pixels)
    grad_flat = cotangent.reshape(chans, feats, pixels)
    device = lax.axis_index("chan")
    start = device * chans
    own = lax.dynamic_slice_in_dim(freq_table, start, chans) // n_chan
    order = jnp.zeros((chans,), jnp.int32).at[own].set(jnp.arange(chans, dtype=jnp.int32))
    h_sorted = hidden_flat[order]
    g_sorted = grad_flat[order]
    h_taps = [h_sorted] * taps
    h_received = []
    g_taps = [g_sorted] * taps
    for dist in range(1, half + 1):
        for sign in (-1, 1):
            h_far = passed_along(h_sorted, "chan", -sign * dist)
            h_received.append(h_far)
            g_far = passed_along(g_sorted, "chan", -sign * dist)
            if sign < 0:
                wrapped = device < dist
                h_near = jnp.where(wrapped, move_down(h_far), h_far)
                g_near = jnp.where(wrapped, move_down(g_far), g_far)
            else:
                wrapped = device + dist >= n_chan
                h_near = jnp.where(wrapped, move_up(h_far), h_far)
                g_near = jnp.where(wrapped, move_up(g_far), g_far)
            h_taps[half + sign * dist] = h_near
            g_taps[half + sign * dist] = g_near
    h_stack = jnp.stack(h_taps, 1).reshape(chans, taps * feats, pixels)
    g_stack = jnp.stack(g_taps, 1).reshape(chans, taps * feats, pixels)
    fwd_weight = spectral_kernel.transpose(1, 0, 2).reshape(feats, taps * feats)
    bwd_weight = spectral_kernel[::-1].transpose(2, 0, 1).reshape(feats, taps * feats)
    fwd_acc = jnp.einsum("gK,mKp->mgp", fwd_weight, h_stack, preferred_element_type=jnp.float32)
    bwd_acc = jnp.einsum("fK,mKp->mfp", bwd_weight, g_stack, preferred_element_type=jnp.float32)
    spec_grad = jnp.einsum(
        "mKp,mfp->Kf", g_stack, h_sorted, preferred_element_type=jnp.float32
    ).reshape(taps, feats, feats)[::-1]
    spec_flat = fwd_acc.astype(jnp.bfloat16)[own]
    back_flat = bwd_acc.astype(jnp.bfloat16)[own]
    spec = spec_flat.reshape(chans, feats, rows, cols)
    back = back_flat.reshape(chans, feats, rows, cols)
    restored = (dirty.astype(jnp.float32) + spec.astype(jnp.float32)).astype(jnp.bfloat16)
    dmixed = (back.astype(jnp.float32) * silu_slope(mixed)).astype(jnp.bfloat16)
    mix_term = jnp.einsum("cghw,cfhw->gf", dmixed, smooth, preferred_element_type=jnp.float32)
    dsmooth = jnp.einsum(
        "gf,cghw->cfhw", feature_mix, dmixed, preferred_element_type=jnp.float32
    ).astype(jnp.bfloat16)
    grad_ext = padded(dsmooth, ((("tile", "sub"), 2),), 2)
    dpad32 = jnp.pad(grad_ext, ((0, 0), (0, 0), (0, 0), (2, 2))).astype(jnp.float32)
    conv = jnp.zeros(dirty.shape, jnp.float32)
    terms = []
    for i in range(5):
        for j in range(5):
            conv = (
                conv
                + spatial_kernel[:, i * 5 + j][None, :, None, None]
                * dpad32[:, :, 4 - i : 4 - i + rows, 4 - j : 4 - j + cols]
            )
            terms.append(
                jnp.einsum(
                    "cfhw,cfhw->f",
                    dsmooth,
                    xpad[:, :, i : i + rows, j : j + cols],
                    preferred_element_type=jnp.float32,
                )
            )
    kernel_term = jnp.stack(terms, 1)
    dirty_grad = (cotangent.astype(jnp.float32) + conv).astype(jnp.bfloat16)
    late = all_summed(kernel_term.reshape(-1) * scale, ("sub", "tile"))
    early = jnp.concatenate([mix_term.reshape(-1), spec_grad.reshape(-1)]) * scale
    early = all_summed(early, ("sub", "tile"))
    flat = all_summed(jnp.concatenate([late, early]), ("chan",), tied=h_received, tie_at=0)
    kgrad = flat[: kernel_term.size].reshape(kernel_term.shape)
    mgrad = flat[kernel_term.size : kernel_term.size + mix_term.size].reshape(mix_term.shape)
    sgrad = flat[kernel_term.size + mix_term.size :].reshape(spec_grad.shape)
    return (restored, dirty_grad, kgrad, mgrad, sgrad)


def solution(mesh):
    in_specs = (
        P(("grp", "chan"), None, ("tile", "sub"), None),
        P(("grp", "chan"), None, ("tile", "sub"), None),
        P(),
        P(),
        P(),
        P(),
    )
    out_specs = (
        P(("grp", "chan"), None, ("tile", "sub"), None),
        P(("grp", "chan"), None, ("tile", "sub"), None),
        P("grp", None),
        P("grp", None),
        P("grp", None, None),
    )
    return jax.shard_map(local, mesh=mesh, in_specs=in_specs, out_specs=out_specs, check_vma=False)
```

```python
import math

import jax
import jax.numpy as jnp
from jax import lax
from jax.sharding import PartitionSpec as P


def padded(block, sides, width):
    for axis, dim in sides:
        count = lax.axis_size(axis)
        forward = [(i, i + 1) for i in range(count - 1)]
        backward = [(target, source) for source, target in forward]
        low = lax.ppermute(
            lax.slice_in_dim(block, block.shape[dim] - width, None, axis=dim), axis, forward
        )
        high = lax.ppermute(lax.slice_in_dim(block, 0, width, axis=dim), axis, backward)
        block = jnp.concatenate([low, block, high], axis=dim)
    return block


def passed_along(block, axis, distance):
    devices = range(lax.axis_size(axis))
    route = [((i - distance) % len(devices), i) for i in devices]
    return lax.ppermute(block, axis, route)


def all_summed(value, axes, tied=None, tie_at=0):
    done = 0
    for axis in axes:
        count = lax.axis_size(axis)
        if count & (count - 1):
            value = lax.psum(value, axis)
            continue
        step = 1
        while step < count:
            if tied is not None and done == tie_at:
                value, _ = lax.optimization_barrier((value, tied))
            value = value + lax.ppermute(value, axis, [(i, i ^ step) for i in range(count)])
            step *= 2
            done += 1
    return value


def silu_slope(value):
    sig = jax.nn.sigmoid(value)
    return sig * (1.0 + value * (1.0 - sig))


def order_of(inverse, source, chans, n_chan):
    table = inverse.reshape(chans, n_chan)
    return lax.dynamic_index_in_dim(table, source, 1, keepdims=False) - source * chans


def move_down(array):
    return jnp.pad(array, ((1, 0), (0, 0), (0, 0)))[:-1]


def move_up(array):
    return jnp.pad(array, ((0, 1), (0, 0), (0, 0)))[1:]


def local(dirty, cotangent, spatial_kernel, feature_mix, spectral_kernel, freq_table):
    chans, feats, rows, cols = dirty.shape
    taps = spectral_kernel.shape[0]
    half = (taps - 1) // 2
    n_chan = lax.axis_size("chan")
    n_rows = lax.axis_size("tile") * lax.axis_size("sub")
    scale = 1.0 / math.sqrt(chans * n_chan * rows * n_rows * cols)
    pixels = rows * cols
    extended = padded(dirty, ((("tile", "sub"), 2),), 2)
    xpad = jnp.pad(extended, ((0, 0), (0, 0), (0, 0), (2, 2)))
    xpad32 = xpad.astype(jnp.float32)
    total = jnp.zeros(dirty.shape, jnp.float32)
    for i in range(5):
        for j in range(5):
            total = (
                total
                + spatial_kernel[:, i * 5 + j][None, :, None, None]
                * xpad32[:, :, i : i + rows, j : j + cols]
            )
    smooth = total.astype(jnp.bfloat16)
    mixed = jnp.einsum("gf,cfhw->cghw", feature_mix, smooth, preferred_element_type=jnp.float32)
    hidden = jax.nn.silu(mixed).astype(jnp.bfloat16)
    hidden_flat = hidden.reshape(chans, feats, pixels)
    grad_flat = cotangent.reshape(chans, feats, pixels)
    device = lax.axis_index("chan")
    start = device * chans
    own = lax.dynamic_slice_in_dim(freq_table, start, chans) // n_chan
    total_chans = freq_table.shape[0]
    inverse = jnp.zeros((total_chans,), jnp.int32).at[freq_table].set(
        jnp.arange(total_chans, dtype=jnp.int32)
    )
    order = order_of(inverse, device, chans, n_chan)
    h_sorted = hidden_flat[order]
    g_sorted = grad_flat[order]
    h_taps = [h_sorted] * taps
    h_received = []
    g_taps = [g_sorted] * taps
    for dist in range(1, half + 1):
        for sign in (-1, 1):
            h_far = passed_along(h_sorted, "chan", -sign * dist)
            h_received.append(h_far)
            g_far = passed_along(grad_flat, "chan", -sign * dist)
            g_far = g_far[order_of(inverse, (device + sign * dist) % n_chan, chans, n_chan)]
            if sign < 0:
                wrapped = device < dist
                h_near = jnp.where(wrapped, move_down(h_far), h_far)
                g_near = jnp.where(wrapped, move_down(g_far), g_far)
            else:
                wrapped = device + dist >= n_chan
                h_near = jnp.where(wrapped, move_up(h_far), h_far)
                g_near = jnp.where(wrapped, move_up(g_far), g_far)
            h_taps[half + sign * dist] = h_near
            g_taps[half + sign * dist] = g_near
    h_stack = jnp.stack(h_taps, 1).reshape(chans, taps * feats, pixels)
    g_stack = jnp.stack(g_taps, 1).reshape(chans, taps * feats, pixels)
    fwd_weight = spectral_kernel.transpose(1, 0, 2).reshape(feats, taps * feats)
    bwd_weight = spectral_kernel[::-1].transpose(2, 0, 1).reshape(feats, taps * feats)
    fwd_acc = jnp.einsum("gK,mKp->mgp", fwd_weight, h_stack, preferred_element_type=jnp.float32)
    bwd_acc = jnp.einsum("fK,mKp->mfp", bwd_weight, g_stack, preferred_element_type=jnp.float32)
    spec_grad = jnp.einsum(
        "mKp,mfp->Kf", g_stack, h_sorted, preferred_element_type=jnp.float32
    ).reshape(taps, feats, feats)[::-1]
    spec_flat = fwd_acc.astype(jnp.bfloat16)[own]
    back_flat = bwd_acc.astype(jnp.bfloat16)[own]
    spec = spec_flat.reshape(chans, feats, rows, cols)
    back = back_flat.reshape(chans, feats, rows, cols)
    restored = (dirty.astype(jnp.float32) + spec.astype(jnp.float32)).astype(jnp.bfloat16)
    dmixed = (back.astype(jnp.float32) * silu_slope(mixed)).astype(jnp.bfloat16)
    mix_term = jnp.einsum("cghw,cfhw->gf", dmixed, smooth, preferred_element_type=jnp.float32)
    dsmooth = jnp.einsum(
        "gf,cghw->cfhw", feature_mix, dmixed, preferred_element_type=jnp.float32
    ).astype(jnp.bfloat16)
    grad_ext = padded(dsmooth, ((("tile", "sub"), 2),), 2)
    dpad32 = jnp.pad(grad_ext, ((0, 0), (0, 0), (0, 0), (2, 2))).astype(jnp.float32)
    conv = jnp.zeros(dirty.shape, jnp.float32)
    terms = []
    for i in range(5):
        for j in range(5):
            conv = (
                conv
                + spatial_kernel[:, i * 5 + j][None, :, None, None]
                * dpad32[:, :, 4 - i : 4 - i + rows, 4 - j : 4 - j + cols]
            )
            terms.append(
                jnp.einsum(
                    "cfhw,cfhw->f",
                    dsmooth,
                    xpad[:, :, i : i + rows, j : j + cols],
                    preferred_element_type=jnp.float32,
                )
            )
    kernel_term = jnp.stack(terms, 1)
    dirty_grad = (cotangent.astype(jnp.float32) + conv).astype(jnp.bfloat16)
    parts = (kernel_term, mix_term, spec_grad)
    flat = jnp.concatenate([part.reshape(-1) for part in parts]) * scale
    flat = all_summed(flat, ("sub", "tile", "chan"), tied=h_received, tie_at=3)
    sizes = [part.size for part in parts]
    kgrad, mgrad, sgrad = (
        piece.reshape(part.shape)
        for piece, part in zip(jnp.split(flat, [sizes[0], sizes[0] + sizes[1]]), parts)
    )
    return (restored, dirty_grad, kgrad, mgrad, sgrad)


def solution(mesh):
    in_specs = (
        P(("grp", "chan"), None, ("tile", "sub"), None),
        P(("grp", "chan"), None, ("tile", "sub"), None),
        P(),
        P(),
        P(),
        P(),
    )
    out_specs = (
        P(("grp", "chan"), None, ("tile", "sub"), None),
        P(("grp", "chan"), None, ("tile", "sub"), None),
        P("grp", None),
        P("grp", None),
        P("grp", None, None),
    )
    return jax.shard_map(local, mesh=mesh, in_specs=in_specs, out_specs=out_specs, check_vma=False)
```

```python
import math

import jax
import jax.numpy as jnp
from jax import lax
from jax.sharding import PartitionSpec as P


def padded(block, sides, width):
    for axis, dim in sides:
        count = lax.axis_size(axis)
        forward = [(i, i + 1) for i in range(count - 1)]
        backward = [(target, source) for source, target in forward]
        low = lax.ppermute(
            lax.slice_in_dim(block, block.shape[dim] - width, None, axis=dim), axis, forward
        )
        high = lax.ppermute(lax.slice_in_dim(block, 0, width, axis=dim), axis, backward)
        block = jnp.concatenate([low, block, high], axis=dim)
    return block


def passed_along(block, axis, distance):
    devices = range(lax.axis_size(axis))
    route = [((i - distance) % len(devices), i) for i in devices]
    return lax.ppermute(block, axis, route)


def all_summed(value, axes, tied=None, tie_at=0):
    done = 0
    for axis in axes:
        count = lax.axis_size(axis)
        if count & (count - 1):
            value = lax.psum(value, axis)
            continue
        step = 1
        while step < count:
            if tied is not None and done == tie_at:
                value, _ = lax.optimization_barrier((value, tied))
            value = value + lax.ppermute(value, axis, [(i, i ^ step) for i in range(count)])
            step *= 2
            done += 1
    return value


def silu_slope(value):
    sig = jax.nn.sigmoid(value)
    return sig * (1.0 + value * (1.0 - sig))


def move_down(array):
    return jnp.pad(array, ((1, 0), (0, 0), (0, 0)))[:-1]


def move_up(array):
    return jnp.pad(array, ((0, 1), (0, 0), (0, 0)))[1:]


def local(dirty, cotangent, spatial_kernel, feature_mix, spectral_kernel, freq_table):
    chans, feats, rows, cols = dirty.shape
    taps = spectral_kernel.shape[0]
    half = (taps - 1) // 2
    n_chan = lax.axis_size("chan")
    n_rows = lax.axis_size("tile") * lax.axis_size("sub")
    scale = 1.0 / math.sqrt(chans * n_chan * rows * n_rows * cols)
    pixels = rows * cols
    extended = padded(dirty, ((("tile", "sub"), 2),), 2)
    xpad = jnp.pad(extended, ((0, 0), (0, 0), (0, 0), (2, 2)))
    xpad32 = xpad.astype(jnp.float32)
    total = jnp.zeros(dirty.shape, jnp.float32)
    for i in range(5):
        for j in range(5):
            total = (
                total
                + spatial_kernel[:, i * 5 + j][None, :, None, None]
                * xpad32[:, :, i : i + rows, j : j + cols]
            )
    smooth = total.astype(jnp.bfloat16)
    mixed = jnp.einsum("gf,cfhw->cghw", feature_mix, smooth, preferred_element_type=jnp.float32)
    hidden = jax.nn.silu(mixed).astype(jnp.bfloat16)
    hidden_flat = hidden.reshape(chans, feats, pixels)
    grad_flat = cotangent.reshape(chans, feats, pixels)
    device = lax.axis_index("chan")
    start = device * chans
    own = lax.dynamic_slice_in_dim(freq_table, start, chans) // n_chan
    slots = jnp.arange(chans, dtype=jnp.int32)
    order = jnp.sum(jnp.where(own[None, :] == slots[:, None], slots[None, :], 0), axis=1)
    h_sorted = hidden_flat[order]
    g_sorted = grad_flat[order]
    h_taps = [h_sorted] * taps
    h_received = []
    g_taps = [g_sorted] * taps
    for dist in range(1, half + 1):
        for sign in (-1, 1):
            h_far = passed_along(h_sorted, "chan", -sign * dist)
            h_received.append(h_far)
            g_far = passed_along(g_sorted, "chan", -sign * dist)
            if sign < 0:
                wrapped = device < dist
                h_near = jnp.where(wrapped, move_down(h_far), h_far)
                g_near = jnp.where(wrapped, move_down(g_far), g_far)
            else:
                wrapped = device + dist >= n_chan
                h_near = jnp.where(wrapped, move_up(h_far), h_far)
                g_near = jnp.where(wrapped, move_up(g_far), g_far)
            h_taps[half + sign * dist] = h_near
            g_taps[half + sign * dist] = g_near
    h_stack = jnp.stack(h_taps, 1).reshape(chans, taps * feats, pixels)
    g_stack = jnp.stack(g_taps, 1).reshape(chans, taps * feats, pixels)
    fwd_weight = spectral_kernel.transpose(1, 0, 2).reshape(feats, taps * feats)
    bwd_weight = spectral_kernel[::-1].transpose(2, 0, 1).reshape(feats, taps * feats)
    fwd_acc = jnp.einsum("gK,mKp->mgp", fwd_weight, h_stack, preferred_element_type=jnp.float32)
    bwd_acc = jnp.einsum("fK,mKp->mfp", bwd_weight, g_stack, preferred_element_type=jnp.float32)
    spec_grad = jnp.einsum(
        "mKp,mfp->Kf", g_stack, h_sorted, preferred_element_type=jnp.float32
    ).reshape(taps, feats, feats)[::-1]
    spec_flat = fwd_acc.astype(jnp.bfloat16)[own]
    back_flat = bwd_acc.astype(jnp.bfloat16)[own]
    spec = spec_flat.reshape(chans, feats, rows, cols)
    back = back_flat.reshape(chans, feats, rows, cols)
    restored = (dirty.astype(jnp.float32) + spec.astype(jnp.float32)).astype(jnp.bfloat16)
    dmixed = (back.astype(jnp.float32) * silu_slope(mixed)).astype(jnp.bfloat16)
    mix_term = jnp.einsum("cghw,cfhw->gf", dmixed, smooth, preferred_element_type=jnp.float32)
    dsmooth = jnp.einsum(
        "gf,cghw->cfhw", feature_mix, dmixed, preferred_element_type=jnp.float32
    ).astype(jnp.bfloat16)
    grad_ext = padded(dsmooth, ((("tile", "sub"), 2),), 2)
    dpad32 = jnp.pad(grad_ext, ((0, 0), (0, 0), (0, 0), (2, 2))).astype(jnp.float32)
    conv = jnp.zeros(dirty.shape, jnp.float32)
    terms = []
    for i in range(5):
        for j in range(5):
            conv = (
                conv
                + spatial_kernel[:, i * 5 + j][None, :, None, None]
                * dpad32[:, :, 4 - i : 4 - i + rows, 4 - j : 4 - j + cols]
            )
            terms.append(
                jnp.einsum(
                    "cfhw,cfhw->f",
                    dsmooth,
                    xpad[:, :, i : i + rows, j : j + cols],
                    preferred_element_type=jnp.float32,
                )
            )
    kernel_term = jnp.stack(terms, 1)
    dirty_grad = (cotangent.astype(jnp.float32) + conv).astype(jnp.bfloat16)
    parts = (kernel_term, mix_term, spec_grad)
    flat = jnp.concatenate([part.reshape(-1) for part in parts]) * scale
    flat = all_summed(flat, ("sub", "tile", "chan"), tied=h_received, tie_at=3)
    sizes = [part.size for part in parts]
    kgrad, mgrad, sgrad = (
        piece.reshape(part.shape)
        for piece, part in zip(jnp.split(flat, [sizes[0], sizes[0] + sizes[1]]), parts)
    )
    return (restored, dirty_grad, kgrad, mgrad, sgrad)


def solution(mesh):
    in_specs = (
        P(("grp", "chan"), None, ("tile", "sub"), None),
        P(("grp", "chan"), None, ("tile", "sub"), None),
        P(),
        P(),
        P(),
        P(),
    )
    out_specs = (
        P(("grp", "chan"), None, ("tile", "sub"), None),
        P(("grp", "chan"), None, ("tile", "sub"), None),
        P("grp", None),
        P("grp", None),
        P("grp", None, None),
    )
    return jax.shard_map(local, mesh=mesh, in_specs=in_specs, out_specs=out_specs, check_vma=False)
```

```python
import math

import jax
import jax.numpy as jnp
from jax import lax
from jax.experimental.layout import Layout, with_layout_constraint
from jax.sharding import PartitionSpec as P


def padded(block, sides, width):
    for axis, dim in sides:
        count = lax.axis_size(axis)
        forward = [(i, i + 1) for i in range(count - 1)]
        backward = [(target, source) for source, target in forward]
        low = lax.ppermute(
            lax.slice_in_dim(block, block.shape[dim] - width, None, axis=dim), axis, forward
        )
        high = lax.ppermute(lax.slice_in_dim(block, 0, width, axis=dim), axis, backward)
        block = jnp.concatenate([low, block, high], axis=dim)
    return block


def passed_along(block, axis, distance):
    devices = range(lax.axis_size(axis))
    route = [((i - distance) % len(devices), i) for i in devices]
    return lax.ppermute(block, axis, route)


def all_summed(value, axes, tied=None, tie_at=0):
    done = 0
    for axis in axes:
        count = lax.axis_size(axis)
        if count & (count - 1):
            value = lax.psum(value, axis)
            continue
        step = 1
        while step < count:
            if tied is not None and done == tie_at:
                value, _ = lax.optimization_barrier((value, tied))
            value = value + lax.ppermute(value, axis, [(i, i ^ step) for i in range(count)])
            step *= 2
            done += 1
    return value


def silu_slope(value):
    sig = jax.nn.sigmoid(value)
    return sig * (1.0 + value * (1.0 - sig))


def move_down(array):
    return jnp.pad(array, ((1, 0), (0, 0), (0, 0)))[:-1]


def move_up(array):
    return jnp.pad(array, ((0, 1), (0, 0), (0, 0)))[1:]


def local(dirty, cotangent, spatial_kernel, feature_mix, spectral_kernel, freq_table):
    chans, feats, rows, cols = dirty.shape
    taps = spectral_kernel.shape[0]
    half = (taps - 1) // 2
    n_chan = lax.axis_size("chan")
    n_rows = lax.axis_size("tile") * lax.axis_size("sub")
    scale = 1.0 / math.sqrt(chans * n_chan * rows * n_rows * cols)
    pixels = rows * cols
    extended = padded(dirty, ((("tile", "sub"), 2),), 2)
    xpad = jnp.pad(extended, ((0, 0), (0, 0), (0, 0), (2, 2)))
    xpad32 = xpad.astype(jnp.float32)
    total = jnp.zeros(dirty.shape, jnp.float32)
    for i in range(5):
        for j in range(5):
            total = (
                total
                + spatial_kernel[:, i * 5 + j][None, :, None, None]
                * xpad32[:, :, i : i + rows, j : j + cols]
            )
    smooth = total.astype(jnp.bfloat16)
    mixed = jnp.einsum("gf,cfhw->cghw", feature_mix, smooth, preferred_element_type=jnp.float32)
    hidden = jax.nn.silu(mixed).astype(jnp.bfloat16)
    hidden_flat = hidden.reshape(chans, feats, pixels)
    grad_flat = cotangent.reshape(chans, feats, pixels)
    device = lax.axis_index("chan")
    start = device * chans
    own = lax.dynamic_slice_in_dim(freq_table, start, chans) // n_chan
    slots = jnp.arange(chans, dtype=jnp.int32)
    order = jnp.sum(jnp.where(own[None, :] == slots[:, None], slots[None, :], 0), axis=1)
    h_sorted = hidden_flat[order]
    g_sorted = grad_flat[order]
    h_taps = [h_sorted] * taps
    h_received = []
    g_taps = [g_sorted] * taps
    for dist in range(1, half + 1):
        for sign in (-1, 1):
            h_far = passed_along(h_sorted, "chan", -sign * dist)
            h_received.append(h_far)
            g_far = passed_along(g_sorted, "chan", -sign * dist)
            if sign < 0:
                wrapped = device < dist
                h_near = jnp.where(wrapped, move_down(h_far), h_far)
                g_near = jnp.where(wrapped, move_down(g_far), g_far)
            else:
                wrapped = device + dist >= n_chan
                h_near = jnp.where(wrapped, move_up(h_far), h_far)
                g_near = jnp.where(wrapped, move_up(g_far), g_far)
            h_taps[half + sign * dist] = h_near
            g_taps[half + sign * dist] = g_near
    h_stack = jnp.stack(h_taps, 1).reshape(chans, taps * feats, pixels)
    g_stack = jnp.stack(g_taps, 1).reshape(chans, taps * feats, pixels)
    fwd_weight = spectral_kernel.transpose(1, 0, 2).reshape(feats, taps * feats)
    bwd_weight = spectral_kernel[::-1].transpose(2, 0, 1).reshape(feats, taps * feats)
    fwd_acc = jnp.einsum("gK,mKp->mgp", fwd_weight, h_stack, preferred_element_type=jnp.float32)
    bwd_acc = jnp.einsum("fK,mKp->mfp", bwd_weight, g_stack, preferred_element_type=jnp.float32)
    spec_grad = jnp.einsum(
        "mKp,mfp->Kf", g_stack, h_sorted, preferred_element_type=jnp.float32
    ).reshape(taps, feats, feats)[::-1]
    spec_flat = fwd_acc.astype(jnp.bfloat16)[own]
    back_flat = bwd_acc.astype(jnp.bfloat16)[own]
    spec = spec_flat.reshape(chans, feats, rows, cols)
    back = back_flat.reshape(chans, feats, rows, cols)
    restored = (dirty.astype(jnp.float32) + spec.astype(jnp.float32)).astype(jnp.bfloat16)
    dmixed = (back.astype(jnp.float32) * silu_slope(mixed)).astype(jnp.bfloat16)
    mix_term = jnp.einsum("cghw,cfhw->gf", dmixed, smooth, preferred_element_type=jnp.float32)
    dsmooth = jnp.einsum(
        "gf,cghw->cfhw", feature_mix, dmixed, preferred_element_type=jnp.float32
    ).astype(jnp.bfloat16)
    grad_ext = padded(dsmooth, ((("tile", "sub"), 2),), 2)
    dpad32 = jnp.pad(grad_ext, ((0, 0), (0, 0), (0, 0), (2, 2))).astype(jnp.float32)
    conv = jnp.zeros(dirty.shape, jnp.float32)
    terms = []
    for i in range(5):
        for j in range(5):
            conv = (
                conv
                + spatial_kernel[:, i * 5 + j][None, :, None, None]
                * dpad32[:, :, 4 - i : 4 - i + rows, 4 - j : 4 - j + cols]
            )
            terms.append(
                jnp.einsum(
                    "cfhw,cfhw->f",
                    dsmooth,
                    xpad[:, :, i : i + rows, j : j + cols],
                    preferred_element_type=jnp.float32,
                )
            )
    kernel_term = jnp.stack(terms, 1)
    dirty_grad = (cotangent.astype(jnp.float32) + conv).astype(jnp.bfloat16)
    dirty_grad = with_layout_constraint(dirty_grad, Layout((0, 1, 2, 3)))
    parts = (kernel_term, mix_term, spec_grad)
    flat = jnp.concatenate([part.reshape(-1) for part in parts]) * scale
    flat = all_summed(flat, ("sub", "tile", "chan"), tied=h_received, tie_at=3)
    sizes = [part.size for part in parts]
    kgrad, mgrad, sgrad = (
        piece.reshape(part.shape)
        for piece, part in zip(jnp.split(flat, [sizes[0], sizes[0] + sizes[1]]), parts)
    )
    return (restored, dirty_grad, kgrad, mgrad, sgrad)


def solution(mesh):
    in_specs = (
        P(("grp", "chan"), None, ("tile", "sub"), None),
        P(("grp", "chan"), None, ("tile", "sub"), None),
        P(),
        P(),
        P(),
        P(),
    )
    out_specs = (
        P(("grp", "chan"), None, ("tile", "sub"), None),
        P(("grp", "chan"), None, ("tile", "sub"), None),
        P("grp", None),
        P("grp", None),
        P("grp", None, None),
    )
    return jax.shard_map(local, mesh=mesh, in_specs=in_specs, out_specs=out_specs, check_vma=False)
```
